32 devices in a mesh: nets: 8 (over z, x), region: 4 (over y, core).
Axes of the slice: x: 2, y: 2, z: 4, core: 2. Of those that a mesh axis runs over, the one named last changes fastest.
Arguments:
- logits: float32 [8192, 256], P('nets'), may hold values from -24 to 465
- tile_values: bfloat16 [8, 4, 384, 128, 128], P('nets', 'region'), may hold values from 0 to 1
- tile_pattern: int32 [8, 4, 384], P('nets', 'region'), may hold values from 0 to 2047
- tile_edge: int32 [8, 4, 384], P('nets', 'region'), may hold values from 0 to 63
- tile_counts: int32 [8, 4, 8], P('nets', 'region'), may hold values from 12 to 48, as said below
- capacity: int32 [4, 65536], P('region', 'nets'), may hold values from 0 to 2
Outputs:
- logit_grad: float32 [8192, 256], P('nets')
- usage: float32 [4, 65536], P('region', 'nets')
The draws below stay inside these ranges and needn't reach their ends.
Inputs may be any that keep to these rules, and one draw needn't show every extreme that they name: `tile_counts`: each entry is at most 48; in every draw some owner receives 48 live slots from every group of a region, and every group has a full owner in every region.
All inputs are finite; a program needn't handle non-finite values.
Results may differ from the reference program's by a relative error of at most 0.0011.
Values may be sent and summed in bfloat16 or wider, within the bound.
No kernel may reach another device: no remote copies, remote signals or barrier semaphores. Data moves between devices by JAX's collectives and lax.ppermute only.
A program may use at most 64 MiB of HBM per device.

```python
import math
import jax
import jax.numpy as jnp
from jax import lax

K = 256
BLOCK = 128
TILES = 384
EBLK_DEV = 64
GROUPS = 8
REGIONS = 4
SEGMENTS = 8192
PBLK = 2048
SLOT = 48
EDGES = 65536


def draw_logits(key, part):
    keys = jax.random.split(key, 3)
    row_scale = jnp.exp(jax.random.uniform(keys[1], (SEGMENTS, 1), jnp.float32) * math.log(4.0))
    col_scale = jnp.exp(jax.random.uniform(keys[2], (1, K), jnp.float32, math.log(0.5), math.log(1.5)))
    base = jax.random.truncated_normal(keys[0], -4.0, 4.0, (SEGMENTS, K), jnp.float32)
    values = base * row_scale * col_scale
    return values.astype(jnp.float32)


def draw_tile_values(key, part):
    keys = jax.random.split(key, 2)
    level = jnp.exp(-3.0 * jax.random.uniform(keys[1], (GROUPS, REGIONS, TILES, BLOCK, 1), jnp.float32))
    entries = jax.random.uniform(keys[0], (GROUPS, REGIONS, TILES, BLOCK, BLOCK), jnp.float32)
    return (entries * level).astype(jnp.bfloat16)


def draw_tile_counts(key, part):
    keys = jax.random.split(key, 3)
    counts = jax.random.randint(keys[0], (GROUPS, REGIONS, GROUPS), SLOT // 4, SLOT + 1)
    own_full = jax.random.randint(keys[1], (GROUPS, REGIONS, 1), 0, GROUPS)
    all_full = jax.random.randint(keys[2], (1, REGIONS, 1), 0, GROUPS)
    column = jnp.arange(GROUPS, dtype=jnp.int32)[None, None, :]
    counts = jnp.where((column == own_full) | (column == all_full), SLOT, counts)
    return counts.astype(jnp.int32)


def plant(values, own_key, smallest, high):
    longest = values.shape.index(max(values.shape))
    spots = []
    for shift in (0, 1):
        where = [jax.random.randint(jax.random.fold_in(own_key, axis), (), 0, length) for axis, length in enumerate(values.shape)]
        where[longest] = (where[longest] + shift) % values.shape[longest]
        spots.append(tuple(where))
    return values.at[spots[0]].set(smallest).at[spots[1]].set(high)


def setup_inputs(seed: int = 0) -> dict:
    streams_of = jax.random.split(jax.random.key(seed), 7)
    logits = draw_logits(jax.random.fold_in(streams_of[6], 71), 0)
    tile_values = draw_tile_values(jax.random.fold_in(streams_of[6], 71), 0)
    tile_pattern = plant(jax.random.randint(streams_of[2], (GROUPS, REGIONS, TILES), 0, PBLK), jax.random.fold_in(streams_of[2], 1), 0, PBLK - 1).astype(jnp.int32)
    tile_edge = plant(jax.random.randint(streams_of[3], (GROUPS, REGIONS, TILES), 0, EBLK_DEV), jax.random.fold_in(streams_of[3], 1), 0, EBLK_DEV - 1).astype(jnp.int32)
    tile_counts = draw_tile_counts(jax.random.fold_in(streams_of[6], 71), 0)
    capacity = plant(jax.random.randint(streams_of[5], (REGIONS, EDGES), 0, 3), jax.random.fold_in(streams_of[5], 1), 0, 2).astype(jnp.int32)
    return {"logits": logits, "tile_values": tile_values, "tile_pattern": tile_pattern, "tile_edge": tile_edge, "tile_counts": tile_counts, "capacity": capacity}


def reference(logits, tile_values, tile_pattern, tile_edge, tile_counts, capacity):
    probs = jax.nn.softmax(logits, axis=-1)
    probs_half = probs.astype(jnp.bfloat16)
    live_slot = (jnp.arange(SLOT, dtype=jnp.int32)[None, None, None, :] < tile_counts[..., None])
    live_slot = live_slot.reshape(GROUPS, REGIONS, TILES).astype(jnp.float32)
    owner_idx = (jnp.arange(TILES, dtype=jnp.int32) // SLOT).astype(jnp.int32)
    target = (owner_idx[None, None, :] * EBLK_DEV + tile_edge).astype(jnp.int32)
    blocks_half = probs_half.reshape(GROUPS, PBLK, BLOCK)
    region_idx = jnp.broadcast_to(jnp.arange(REGIONS, dtype=jnp.int32)[:, None], (REGIONS, TILES))

    def forward(carry, item):
        values, pattern_idx, target_idx, weight_live, blocks = item
        picked = blocks[pattern_idx].astype(jnp.float32)
        contrib = jnp.einsum("rtq,rtqe->rte", picked, values.astype(jnp.float32)) * weight_live[..., None]
        return carry.at[region_idx, target_idx].add(contrib), None

    start = jnp.zeros((REGIONS, GROUPS * EBLK_DEV, BLOCK), jnp.float32)
    usage_edges, _ = lax.scan(forward, start, (tile_values, tile_pattern, target, live_slot, blocks_half))
    capacity_f = capacity.reshape(REGIONS, GROUPS * EBLK_DEV, BLOCK).astype(jnp.float32)
    edge_grad = jax.nn.sigmoid(usage_edges - capacity_f).astype(jnp.bfloat16)

    def backward(item):
        values, pattern_idx, target_idx, weight_live = item
        slot_grads = edge_grad[region_idx, target_idx].astype(jnp.float32)
        dp_tiles = jnp.einsum("rtqe,rte->rtq", values.astype(jnp.float32), slot_grads) * weight_live[..., None]
        local_grad = jnp.zeros((PBLK, BLOCK), jnp.float32)
        return local_grad.at[pattern_idx.reshape(-1)].add(dp_tiles.reshape(-1, BLOCK))

    grads = lax.map(backward, (tile_values, tile_pattern, target, live_slot))
    summed_grad = grads.reshape(SEGMENTS, K)
    logit_grad = probs * (summed_grad - jnp.sum(probs * summed_grad, axis=-1, keepdims=True))
    return logit_grad, usage_edges.reshape(REGIONS, EDGES)
```

```python
import jax
import jax.numpy as jnp
from jax import lax
from jax.sharding import PartitionSpec as P


def shards(logits, tile_values, tile_pattern, tile_edge, tile_counts, capacity):
    groups = lax.axis_size("nets")
    tile_block = tile_values[0, 0]
    tile_count = tile_block.shape[0]
    block_size = tile_block.shape[1]
    slot_count = tile_count // groups
    pattern_idx = tile_pattern[0, 0]
    edge_idx = tile_edge[0, 0]
    counts = tile_counts[0, 0]
    live_slot = (jnp.arange(slot_count, dtype=jnp.int32)[None, :] < counts[:, None]).reshape(
        tile_count
    )
    weight_live = live_slot.astype(jnp.float32)
    probs = jax.nn.softmax(logits, axis=-1)
    probs_half = probs.astype(jnp.bfloat16).reshape(-1, block_size)
    picked = probs_half[pattern_idx]
    contrib = (
        jnp.einsum("tq,tqe->te", picked, tile_block, preferred_element_type=jnp.float32)
        * weight_live[:, None]
    )
    capacity_f = capacity.reshape(-1, block_size).astype(jnp.float32)
    owned_blocks = capacity_f.shape[0]
    owner_idx = jnp.arange(tile_count, dtype=jnp.int32) // slot_count
    target = owner_idx * owned_blocks + edge_idx
    partial_value = (
        jnp.zeros((groups * owned_blocks, block_size), jnp.float32).at[target].add(contrib)
    )
    received = lax.all_to_all(
        partial_value.reshape(groups, owned_blocks, block_size), "nets", 0, 0, tiled=False
    )
    usage_edges = jnp.sum(received, axis=0)
    edge_grad = jax.nn.sigmoid(usage_edges - capacity_f).astype(jnp.bfloat16)
    spread = jnp.broadcast_to(edge_grad[None], (groups, owned_blocks, block_size))
    all_grads = lax.all_to_all(spread, "nets", 0, 0, tiled=False).reshape(-1, block_size)
    slot_grads = all_grads[target]
    dp_tiles = (
        jnp.einsum("tqe,te->tq", tile_block, slot_grads, preferred_element_type=jnp.float32)
        * weight_live[:, None]
    )
    idx_rows = -(-tile_count // block_size)
    idx_f = jnp.zeros((idx_rows * block_size,), jnp.float32).at[:tile_count].set(
        pattern_idx.astype(jnp.float32)
    )
    packed = jnp.concatenate([dp_tiles, idx_f.reshape(idx_rows, block_size)], axis=0)
    gathered = lax.all_gather(packed, "region", axis=0, tiled=False)
    all_dp = gathered[:, :tile_count].reshape(-1, block_size)
    all_idx = (
        gathered[:, tile_count:].reshape(gathered.shape[0], -1)[:, :tile_count]
        .astype(jnp.int32)
        .reshape(-1)
    )
    summed_grad = (
        jnp.zeros((probs_half.shape[0], block_size), jnp.float32).at[all_idx].add(all_dp)
    ).reshape(logits.shape)
    logit_grad = probs * (summed_grad - jnp.sum(probs * summed_grad, axis=-1, keepdims=True))
    return (logit_grad, usage_edges.reshape(capacity.shape))


def solution(mesh):
    in_specs = (
        P("nets", None),
        P("nets", "region", None, None, None),
        P("nets", "region", None),
        P("nets", "region", None),
        P("nets", "region", None),
        P("region", "nets"),
    )
    out_specs = (P("nets", None), P("region", "nets"))
    return jax.shard_map(shards, mesh=mesh, in_specs=in_specs, out_specs=out_specs, check_vma=False)
```

```python
import jax
import jax.numpy as jnp
from jax import lax
from jax.sharding import PartitionSpec as P


def _one_hot(idx, size, dtype):
    return (idx[:, None] == jnp.arange(size, dtype=jnp.int32)[None, :]).astype(dtype)


def _take_rows(table, idx):
    sel = _one_hot(idx, table.shape[0], table.dtype)
    return jnp.dot(sel, table, preferred_element_type=jnp.float32).astype(table.dtype)


def _add_rows(idx, rows, size):
    hi = lax.reduce_precision(rows, exponent_bits=8, mantissa_bits=7)
    rest = rows - hi
    mid = lax.reduce_precision(rest, exponent_bits=8, mantissa_bits=7)
    lo = rest - mid
    parts = jnp.concatenate([hi, mid, lo], axis=1).astype(jnp.bfloat16)
    sel = _one_hot(idx, size, jnp.bfloat16)
    out = lax.dot_general(
        sel, parts, (((0,), (0,)), ((), ())), preferred_element_type=jnp.float32
    )
    width = rows.shape[1]
    return out[:, :width] + out[:, width : 2 * width] + out[:, 2 * width :]


def shards(logits, tile_values, tile_pattern, tile_edge, tile_counts, capacity):
    groups = lax.axis_size("nets")
    tile_block = tile_values[0, 0]
    tile_count = tile_block.shape[0]
    block_size = tile_block.shape[1]
    slot_count = tile_count // groups
    pattern_idx = tile_pattern[0, 0]
    edge_idx = tile_edge[0, 0]
    counts = tile_counts[0, 0]
    live_slot = (jnp.arange(slot_count, dtype=jnp.int32)[None, :] < counts[:, None]).reshape(
        tile_count
    )
    weight_live = live_slot.astype(jnp.float32)
    probs = jax.nn.softmax(logits, axis=-1)
    probs_half = probs.astype(jnp.bfloat16).reshape(-1, block_size)
    picked = _take_rows(probs_half, pattern_idx)
    contrib = (
        jnp.einsum("tq,tqe->te", picked, tile_block, preferred_element_type=jnp.float32)
        * weight_live[:, None]
    )
    capacity_f = capacity.reshape(-1, block_size).astype(jnp.float32)
    owned_blocks = capacity_f.shape[0]
    owner_idx = jnp.arange(tile_count, dtype=jnp.int32) // slot_count
    target = owner_idx * owned_blocks + edge_idx
    partial_value = _add_rows(target, contrib, groups * owned_blocks)
    received = lax.all_to_all(
        partial_value.reshape(groups, owned_blocks, block_size), "nets", 0, 0, tiled=False
    )
    usage_edges = jnp.sum(received, axis=0)
    edge_grad = jax.nn.sigmoid(usage_edges - capacity_f).astype(jnp.bfloat16)
    spread = jnp.broadcast_to(edge_grad[None], (groups, owned_blocks, block_size))
    all_grads = lax.all_to_all(spread, "nets", 0, 0, tiled=False).reshape(-1, block_size)
    slot_grads = _take_rows(all_grads, target)
    dp_tiles = (
        jnp.einsum("tqe,te->tq", tile_block, slot_grads, preferred_element_type=jnp.float32)
        * weight_live[:, None]
    )
    idx_rows = -(-tile_count // block_size)
    idx_f = jnp.zeros((idx_rows * block_size,), jnp.float32).at[:tile_count].set(
        pattern_idx.astype(jnp.float32)
    )
    packed = jnp.concatenate([dp_tiles, idx_f.reshape(idx_rows, block_size)], axis=0)
    gathered = lax.all_gather(packed, "region", axis=0, tiled=False)
    all_dp = gathered[:, :tile_count].reshape(-1, block_size)
    all_idx = (
        gathered[:, tile_count:].reshape(gathered.shape[0], -1)[:, :tile_count]
        .astype(jnp.int32)
        .reshape(-1)
    )
    summed_grad = _add_rows(all_idx, all_dp, probs_half.shape[0]).reshape(logits.shape)
    logit_grad = probs * (summed_grad - jnp.sum(probs * summed_grad, axis=-1, keepdims=True))
    return (logit_grad, usage_edges.reshape(capacity.shape))


def solution(mesh):
    in_specs = (
        P("nets", None),
        P("nets", "region", None, None, None),
        P("nets", "region", None),
        P("nets", "region", None),
        P("nets", "region", None),
        P("region", "nets"),
    )
    out_specs = (P("nets", None), P("region", "nets"))
    return jax.shard_map(shards, mesh=mesh, in_specs=in_specs, out_specs=out_specs, check_vma=False)
```

```python
import jax
import jax.numpy as jnp
from jax import lax
from jax.sharding import PartitionSpec as P


def _one_hot(idx, size, dtype):
    return (idx[:, None] == jnp.arange(size, dtype=jnp.int32)[None, :]).astype(dtype)


def _take_rows(table, idx):
    sel = _one_hot(idx, table.shape[0], table.dtype)
    return jnp.dot(sel, table, preferred_element_type=jnp.float32).astype(table.dtype)


def _add_rows(idx, rows, size):
    hi = lax.reduce_precision(rows, exponent_bits=8, mantissa_bits=7)
    rest = rows - hi
    mid = lax.reduce_precision(rest, exponent_bits=8, mantissa_bits=7)
    lo = rest - mid
    parts = jnp.concatenate([hi, mid, lo], axis=1).astype(jnp.bfloat16)
    sel = _one_hot(idx, size, jnp.bfloat16)
    out = lax.dot_general(
        sel, parts, (((0,), (0,)), ((), ())), preferred_element_type=jnp.float32
    )
    width = rows.shape[1]
    return out[:, :width] + out[:, width : 2 * width] + out[:, 2 * width :]


def shards(logits, tile_values, tile_pattern, tile_edge, tile_counts, capacity):
    groups = lax.axis_size("nets")
    me = lax.axis_index("nets")
    tile_block = tile_values[0, 0]
    tile_count = tile_block.shape[0]
    block_size = tile_block.shape[1]
    slot_count = tile_count // groups
    pattern_idx = tile_pattern[0, 0]
    edge_idx = tile_edge[0, 0]
    counts = tile_counts[0, 0]
    live_slot = jnp.arange(slot_count, dtype=jnp.int32)[None, :] < counts[:, None]
    weight_live = live_slot.astype(jnp.float32)
    probs = jax.nn.softmax(logits, axis=-1)
    probs_half = probs.astype(jnp.bfloat16).reshape(-1, block_size)
    capacity_f = capacity.reshape(-1, block_size).astype(jnp.float32)
    owned_blocks = capacity_f.shape[0]

    def owner_slots(owner):
        first = owner * slot_count
        tiles = lax.dynamic_slice_in_dim(tile_block, first, slot_count, axis=0)
        patterns = lax.dynamic_slice_in_dim(pattern_idx, first, slot_count, axis=0)
        edges = lax.dynamic_slice_in_dim(edge_idx, first, slot_count, axis=0)
        live = lax.dynamic_index_in_dim(weight_live, owner, axis=0, keepdims=False)
        return tiles, patterns, edges, live

    def owner_partial(owner):
        tiles, patterns, edges, live = owner_slots(owner)
        picked = _take_rows(probs_half, patterns)
        contrib = (
            jnp.einsum("tq,tqe->te", picked, tiles, preferred_element_type=jnp.float32)
            * live[:, None]
        )
        return _add_rows(edges, contrib, owned_blocks)

    usage_edges = None
    for k in list(range(1, groups)) + [0]:
        part = owner_partial((me + k) % groups)
        if k:
            perm = [(s, (s + k) % groups) for s in range(groups)]
            part = lax.ppermute(part, "nets", perm)
        usage_edges = part if usage_edges is None else usage_edges + part
    edge_grad = jax.nn.sigmoid(usage_edges - capacity_f).astype(jnp.bfloat16)

    def owner_terms(owner, grads):
        tiles, patterns, edges, live = owner_slots(owner)
        slot_grads = _take_rows(grads, edges)
        dp = (
            jnp.einsum("tqe,te->tq", tiles, slot_grads, preferred_element_type=jnp.float32)
            * live[:, None]
        )
        return dp, patterns

    dp_parts, idx_parts = [], []
    for k in range(groups):
        grads = edge_grad
        if k:
            perm = [(s, (s + k) % groups) for s in range(groups)]
            grads = lax.ppermute(edge_grad, "nets", perm)
        dp, patterns = owner_terms((me - k) % groups, grads)
        dp_parts.append(dp)
        idx_parts.append(patterns)
    dp_tiles = jnp.concatenate(dp_parts, axis=0)
    order_idx = jnp.concatenate(idx_parts, axis=0)
    idx_rows = -(-tile_count // block_size)
    idx_f = jnp.zeros((idx_rows * block_size,), jnp.float32).at[:tile_count].set(
        order_idx.astype(jnp.float32)
    )
    packed = jnp.concatenate([dp_tiles, idx_f.reshape(idx_rows, block_size)], axis=0)
    gathered = lax.all_gather(packed, "region", axis=0, tiled=False)
    all_dp = gathered[:, :tile_count].reshape(-1, block_size)
    all_idx = (
        gathered[:, tile_count:].reshape(gathered.shape[0], -1)[:, :tile_count]
        .astype(jnp.int32)
        .reshape(-1)
    )
    summed_grad = _add_rows(all_idx, all_dp, probs_half.shape[0]).reshape(logits.shape)
    logit_grad = probs * (summed_grad - jnp.sum(probs * summed_grad, axis=-1, keepdims=True))
    return (logit_grad, usage_edges.reshape(capacity.shape))


def solution(mesh):
    in_specs = (
        P("nets", None),
        P("nets", "region", None, None, None),
        P("nets", "region", None),
        P("nets", "region", None),
        P("nets", "region", None),
        P("region", "nets"),
    )
    out_specs = (P("nets", None), P("region", "nets"))
    return jax.shard_map(shards, mesh=mesh, in_specs=in_specs, out_specs=out_specs, check_vma=False)
```

```python
import jax
import jax.numpy as jnp
from jax import lax
from jax.experimental import pallas as pl
from jax.sharding import PartitionSpec as P


def _one_hot(idx, size, dtype):
    return (idx[:, None] == jnp.arange(size, dtype=jnp.int32)[None, :]).astype(dtype)


def _take_rows(table, idx):
    sel = _one_hot(idx, table.shape[0], table.dtype)
    return jnp.dot(sel, table, preferred_element_type=jnp.float32).astype(table.dtype)


def _add_rows(idx, rows, size):
    hi = lax.reduce_precision(rows, exponent_bits=8, mantissa_bits=7)
    rest = rows - hi
    mid = lax.reduce_precision(rest, exponent_bits=8, mantissa_bits=7)
    lo = rest - mid
    parts = jnp.concatenate([hi, mid, lo], axis=1).astype(jnp.bfloat16)
    sel = _one_hot(idx, size, jnp.bfloat16)
    out = lax.dot_general(
        sel, parts, (((0,), (0,)), ((), ())), preferred_element_type=jnp.float32
    )
    width = rows.shape[1]
    return out[:, :width] + out[:, width : 2 * width] + out[:, 2 * width :]


def _softmax_kernel(x_ref, p_ref, h_ref):
    x = x_ref[...]
    e = jnp.exp(x - jnp.max(x, axis=-1, keepdims=True))
    p = e / jnp.sum(e, axis=-1, keepdims=True)
    p_ref[...] = p
    half = p.astype(jnp.bfloat16)
    width = h_ref.shape[-1]
    for h in range(h_ref.shape[0]):
        h_ref[h] = half[:, h * width : (h + 1) * width]


def _softmax(logits, block_size):
    rows, width = logits.shape
    halves = width // block_size
    step = min(rows, 256)
    return pl.pallas_call(
        _softmax_kernel,
        grid=(rows // step,),
        in_specs=[pl.BlockSpec((step, width), lambda i: (i, 0))],
        out_specs=[
            pl.BlockSpec((step, width), lambda i: (i, 0)),
            pl.BlockSpec((halves, step, block_size), lambda i: (0, i, 0)),
        ],
        out_shape=[
            jax.ShapeDtypeStruct((rows, width), jnp.float32),
            jax.ShapeDtypeStruct((halves, rows, block_size), jnp.bfloat16),
        ],
        cost_estimate=pl.CostEstimate(
            flops=5 * rows * width, transcendentals=rows * width, bytes_accessed=10 * rows * width
        ),
    )(logits)


def shards(logits, tile_values, tile_pattern, tile_edge, tile_counts, capacity):
    groups = lax.axis_size("nets")
    tile_block = tile_values[0, 0]
    tile_count = tile_block.shape[0]
    block_size = tile_block.shape[1]
    slot_count = tile_count // groups
    pattern_idx = tile_pattern[0, 0]
    edge_idx = tile_edge[0, 0]
    counts = tile_counts[0, 0]
    live_slot = (jnp.arange(slot_count, dtype=jnp.int32)[None, :] < counts[:, None]).reshape(
        tile_count
    )
    weight_live = live_slot.astype(jnp.float32)
    probs, probs_split = _softmax(logits, block_size)
    segments, halves = probs_split.shape[1], probs_split.shape[0]
    probs_half = probs_split.reshape(-1, block_size)
    split_idx = (pattern_idx % halves) * segments + pattern_idx // halves
    picked = _take_rows(probs_half, split_idx)
    contrib = (
        jnp.einsum("tq,tqe->te", picked, tile_block, preferred_element_type=jnp.float32)
        * weight_live[:, None]
    )
    capacity_f = capacity.reshape(-1, block_size).astype(jnp.float32)
    owned_blocks = capacity_f.shape[0]
    owner_idx = jnp.arange(tile_count, dtype=jnp.int32) // slot_count
    target = owner_idx * owned_blocks + edge_idx
    partial_value = _add_rows(target, contrib, groups * owned_blocks)
    received = lax.all_to_all(
        partial_value.reshape(groups, owned_blocks, block_size), "nets", 0, 0, tiled=False
    )
    usage_edges = jnp.sum(received, axis=0)
    edge_grad = jax.nn.sigmoid(usage_edges - capacity_f).astype(jnp.bfloat16)
    spread = jnp.broadcast_to(edge_grad[None], (groups, owned_blocks, block_size))
    all_grads = lax.all_to_all(spread, "nets", 0, 0, tiled=False).reshape(-1, block_size)
    slot_grads = _take_rows(all_grads, target)
    dp_tiles = (
        jnp.einsum("tqe,te->tq", tile_block, slot_grads, preferred_element_type=jnp.float32)
        * weight_live[:, None]
    )
    idx_rows = -(-tile_count // block_size)
    idx_f = jnp.zeros((idx_rows * block_size,), jnp.float32).at[:tile_count].set(
        split_idx.astype(jnp.float32)
    )
    packed = jnp.concatenate([dp_tiles, idx_f.reshape(idx_rows, block_size)], axis=0)
    gathered = lax.all_gather(packed, "region", axis=0, tiled=False)
    all_dp = gathered[:, :tile_count].reshape(-1, block_size)
    all_idx = (
        gathered[:, tile_count:].reshape(gathered.shape[0], -1)[:, :tile_count]
        .astype(jnp.int32)
        .reshape(-1)
    )
    summed = _add_rows(all_idx, all_dp, probs_half.shape[0]).reshape(halves, segments, block_size)
    summed_grad = jnp.concatenate([summed[h] for h in range(halves)], axis=1)
    logit_grad = probs * (summed_grad - jnp.sum(probs * summed_grad, axis=-1, keepdims=True))
    return (logit_grad, usage_edges.reshape(capacity.shape))


def solution(mesh):
    in_specs = (
        P("nets", None),
        P("nets", "region", None, None, None),
        P("nets", "region", None),
        P("nets", "region", None),
        P("nets", "region", None),
        P("region", "nets"),
    )
    out_specs = (P("nets", None), P("region", "nets"))
    return jax.shard_map(shards, mesh=mesh, in_specs=in_specs, out_specs=out_specs, check_vma=False)
```

```python
import jax
import jax.numpy as jnp
from jax import lax
from jax.experimental import pallas as pl
from jax.sharding import PartitionSpec as P


def _one_hot(idx, size, dtype):
    return (idx[:, None] == jnp.arange(size, dtype=jnp.int32)[None, :]).astype(dtype)


def _take_rows(table, idx):
    sel = _one_hot(idx, table.shape[0], table.dtype)
    return jnp.dot(sel, table, preferred_element_type=jnp.float32).astype(table.dtype)


def _add_rows(idx, rows, size):
    hi = lax.reduce_precision(rows, exponent_bits=8, mantissa_bits=7)
    rest = rows - hi
    mid = lax.reduce_precision(rest, exponent_bits=8, mantissa_bits=7)
    lo = rest - mid
    parts = jnp.concatenate([hi, mid, lo], axis=1).astype(jnp.bfloat16)
    sel = _one_hot(idx, size, jnp.bfloat16)
    out = lax.dot_general(
        sel, parts, (((0,), (0,)), ((), ())), preferred_element_type=jnp.float32
    )
    width = rows.shape[1]
    return out[:, :width] + out[:, width : 2 * width] + out[:, 2 * width :]


def _softmax_kernel(x_ref, p_ref, h_ref):
    x = x_ref[...]
    e = jnp.exp(x - jnp.max(x, axis=-1, keepdims=True))
    p = e * (1.0 / jnp.sum(e, axis=-1, keepdims=True))
    p_ref[...] = p
    half = p.astype(jnp.bfloat16)
    width = h_ref.shape[-1]
    for h in range(h_ref.shape[0]):
        h_ref[h] = half[:, h * width : (h + 1) * width]


def _softmax(logits, block_size):
    rows, width = logits.shape
    halves = width // block_size
    step = min(rows, 512)
    return pl.pallas_call(
        _softmax_kernel,
        grid=(rows // step,),
        in_specs=[pl.BlockSpec((step, width), lambda i: (i, 0))],
        out_specs=[
            pl.BlockSpec((step, width), lambda i: (i, 0)),
            pl.BlockSpec((halves, step, block_size), lambda i: (0, i, 0)),
        ],
        out_shape=[
            jax.ShapeDtypeStruct((rows, width), jnp.float32),
            jax.ShapeDtypeStruct((halves, rows, block_size), jnp.bfloat16),
        ],
        cost_estimate=pl.CostEstimate(
            flops=5 * rows * width, transcendentals=rows * width, bytes_accessed=10 * rows * width
        ),
    )(logits)


def shards(logits, tile_values, tile_pattern, tile_edge, tile_counts, capacity):
    groups = lax.axis_size("nets")
    tile_block = tile_values[0, 0]
    tile_count = tile_block.shape[0]
    block_size = tile_block.shape[1]
    slot_count = tile_count // groups
    pattern_idx = tile_pattern[0, 0]
    edge_idx = tile_edge[0, 0]
    counts = tile_counts[0, 0]
    live_slot = (jnp.arange(slot_count, dtype=jnp.int32)[None, :] < counts[:, None]).reshape(
        tile_count
    )
    weight_live = live_slot.astype(jnp.float32)
    probs, probs_split = _softmax(logits, block_size)
    segments, halves = probs_split.shape[1], probs_split.shape[0]
    probs_half = probs_split.reshape(-1, block_size)
    split_idx = lax.optimization_barrier((pattern_idx % halves) * segments + pattern_idx // halves)
    picked = _take_rows(probs_half, split_idx)
    contrib = (
        jnp.einsum("tq,tqe->te", picked, tile_block, preferred_element_type=jnp.float32)
        * weight_live[:, None]
    )
    capacity_f = capacity.reshape(-1, block_size).astype(jnp.float32)
    owned_blocks = capacity_f.shape[0]
    owner_idx = jnp.arange(tile_count, dtype=jnp.int32) // slot_count
    target = owner_idx * owned_blocks + edge_idx
    partial_value = _add_rows(target, contrib, groups * owned_blocks)
    received = lax.all_to_all(
        partial_value.reshape(groups, owned_blocks, block_size), "nets", 0, 0, tiled=False
    )
    usage_edges = jnp.sum(received, axis=0)
    edge_grad = jax.nn.sigmoid(usage_edges - capacity_f).astype(jnp.bfloat16)
    spread = jnp.broadcast_to(edge_grad[None], (groups, owned_blocks, block_size))
    all_grads = lax.all_to_all(spread, "nets", 0, 0, tiled=False).reshape(-1, block_size)
    slot_grads = _take_rows(all_grads, target)
    dp_tiles = (
        jnp.einsum("tqe,te->tq", tile_block, slot_grads, preferred_element_type=jnp.float32)
        * weight_live[:, None]
    )
    idx_rows = -(-tile_count // block_size)
    idx_f = jnp.zeros((idx_rows * block_size,), jnp.float32).at[:tile_count].set(
        split_idx.astype(jnp.float32)
    )
    packed = jnp.concatenate([dp_tiles, idx_f.reshape(idx_rows, block_size)], axis=0)
    gathered = lax.all_gather(packed, "region", axis=0, tiled=False)
    all_dp = gathered[:, :tile_count].reshape(-1, block_size)
    all_idx = (
        gathered[:, tile_count:].reshape(gathered.shape[0], -1)[:, :tile_count]
        .astype(jnp.int32)
        .reshape(-1)
    )
    summed = _add_rows(all_idx, all_dp, probs_half.shape[0]).reshape(halves, segments, block_size)
    summed_grad = jnp.concatenate([summed[h] for h in range(halves)], axis=1)
    logit_grad = probs * (summed_grad - jnp.sum(probs * summed_grad, axis=-1, keepdims=True))
    return (logit_grad, usage_edges.reshape(capacity.shape))


def solution(mesh):
    in_specs = (
        P("nets", None),
        P("nets", "region", None, None, None),
        P("nets", "region", None),
        P("nets", "region", None),
        P("nets", "region", None),
        P("region", "nets"),
    )
    out_specs = (P("nets", None), P("region", "nets"))
    return jax.shard_map(shards, mesh=mesh, in_specs=in_specs, out_specs=out_specs, check_vma=False)
```

```python
import jax
import jax.numpy as jnp
from jax import lax
from jax.experimental import pallas as pl
from jax.sharding import PartitionSpec as P


def _one_hot(idx, size, dtype):
    return (idx[:, None] == jnp.arange(size, dtype=jnp.int32)[None, :]).astype(dtype)


def _take_rows(table, idx):
    sel = _one_hot(idx, table.shape[0], table.dtype)
    return jnp.dot(sel, table, preferred_element_type=jnp.float32).astype(table.dtype)


def _add_rows(idx, rows, size):
    hi = lax.reduce_precision(rows, exponent_bits=8, mantissa_bits=7)
    rest = rows - hi
    mid = lax.reduce_precision(rest, exponent_bits=8, mantissa_bits=7)
    lo = rest - mid
    parts = jnp.concatenate([hi, mid, lo], axis=1).astype(jnp.bfloat16)
    sel = _one_hot(idx, size, jnp.bfloat16)
    out = lax.dot_general(
        sel, parts, (((0,), (0,)), ((), ())), preferred_element_type=jnp.float32
    )
    width = rows.shape[1]
    return out[:, :width] + out[:, width : 2 * width] + out[:, 2 * width :]


def _softmax_kernel(x_ref, p_ref, h_ref):
    x = x_ref[...]
    e = jnp.exp(x - jnp.max(x, axis=-1, keepdims=True))
    p = e * (1.0 / jnp.sum(e, axis=-1, keepdims=True))
    p_ref[...] = p
    half = p.astype(jnp.bfloat16)
    width = h_ref.shape[-1]
    for h in range(h_ref.shape[0]):
        h_ref[h] = half[:, h * width : (h + 1) * width]


def _softmax(logits, block_size):
    rows, width = logits.shape
    halves = width // block_size
    step = min(rows, 512)
    return pl.pallas_call(
        _softmax_kernel,
        grid=(rows // step,),
        in_specs=[pl.BlockSpec((step, width), lambda i: (i, 0))],
        out_specs=[
            pl.BlockSpec((step, width), lambda i: (i, 0)),
            pl.BlockSpec((halves, step, block_size), lambda i: (0, i, 0)),
        ],
        out_shape=[
            jax.ShapeDtypeStruct((rows, width), jnp.float32),
            jax.ShapeDtypeStruct((halves, rows, block_size), jnp.bfloat16),
        ],
        cost_estimate=pl.CostEstimate(
            flops=5 * rows * width, transcendentals=rows * width, bytes_accessed=10 * rows * width
        ),
    )(logits)


def shards(logits, tile_values, tile_pattern, tile_edge, tile_counts, capacity):
    groups = lax.axis_size("nets")
    tile_block = tile_values[0, 0]
    tile_count = tile_block.shape[0]
    block_size = tile_block.shape[1]
    slot_count = tile_count // groups
    pattern_idx = tile_pattern[0, 0]
    edge_idx = tile_edge[0, 0]
    counts = tile_counts[0, 0]
    live_slot = (jnp.arange(slot_count, dtype=jnp.int32)[None, :] < counts[:, None]).reshape(
        tile_count
    )
    weight_live = live_slot.astype(jnp.float32)
    probs, probs_split = _softmax(logits, block_size)
    segments, halves = probs_split.shape[1], probs_split.shape[0]
    probs_half = probs_split.reshape(-1, block_size)
    split_idx = lax.optimization_barrier((pattern_idx % halves) * segments + pattern_idx // halves)
    picked = _take_rows(probs_half, split_idx)
    contrib = (
        jnp.sum(picked.astype(jnp.float32)[:, :, None] * tile_block.astype(jnp.float32), axis=1)
        * weight_live[:, None]
    )
    capacity_f = capacity.reshape(-1, block_size).astype(jnp.float32)
    owned_blocks = capacity_f.shape[0]
    owner_idx = jnp.arange(tile_count, dtype=jnp.int32) // slot_count
    target = owner_idx * owned_blocks + edge_idx
    partial_value = _add_rows(target, contrib, groups * owned_blocks)
    received = lax.all_to_all(
        partial_value.reshape(groups, owned_blocks, block_size), "nets", 0, 0, tiled=False
    )
    usage_edges = jnp.sum(received, axis=0)
    edge_grad = jax.nn.sigmoid(usage_edges - capacity_f).astype(jnp.bfloat16)
    spread = jnp.broadcast_to(edge_grad[None], (groups, owned_blocks, block_size))
    all_grads = lax.all_to_all(spread, "nets", 0, 0, tiled=False).reshape(-1, block_size)
    slot_grads = _take_rows(all_grads, target)
    dp_tiles = (
        jnp.sum(tile_block.astype(jnp.float32) * slot_grads.astype(jnp.float32)[:, None, :], axis=2)
        * weight_live[:, None]
    )
    idx_rows = -(-tile_count // block_size)
    idx_f = jnp.zeros((idx_rows * block_size,), jnp.float32).at[:tile_count].set(
        split_idx.astype(jnp.float32)
    )
    packed = jnp.concatenate([dp_tiles, idx_f.reshape(idx_rows, block_size)], axis=0)
    gathered = lax.all_gather(packed, "region", axis=0, tiled=False)
    all_dp = gathered[:, :tile_count].reshape(-1, block_size)
    all_idx = (
        gathered[:, tile_count:].reshape(gathered.shape[0], -1)[:, :tile_count]
        .astype(jnp.int32)
        .reshape(-1)
    )
    summed = _add_rows(all_idx, all_dp, probs_half.shape[0]).reshape(halves, segments, block_size)
    summed_grad = jnp.concatenate([summed[h] for h in range(halves)], axis=1)
    logit_grad = probs * (summed_grad - jnp.sum(probs * summed_grad, axis=-1, keepdims=True))
    return (logit_grad, usage_edges.reshape(capacity.shape))


def solution(mesh):
    in_specs = (
        P("nets", None),
        P("nets", "region", None, None, None),
        P("nets", "region", None),
        P("nets", "region", None),
        P("nets", "region", None),
        P("region", "nets"),
    )
    out_specs = (P("nets", None), P("region", "nets"))
    return jax.shard_map(shards, mesh=mesh, in_specs=in_specs, out_specs=out_specs, check_vma=False)
```

```python
import jax
import jax.numpy as jnp
from jax import lax
from jax.experimental import pallas as pl
from jax.sharding import PartitionSpec as P


def _one_hot(idx, size, dtype):
    return (idx[:, None] == jnp.arange(size, dtype=jnp.int32)[None, :]).astype(dtype)


def _take_rows(table, idx):
    sel = _one_hot(idx, table.shape[0], table.dtype)
    return jnp.dot(sel, table, preferred_element_type=jnp.float32).astype(table.dtype)


def _add_rows(idx, rows, size):
    hi = lax.reduce_precision(rows, exponent_bits=8, mantissa_bits=7)
    rest = rows - hi
    mid = lax.reduce_precision(rest, exponent_bits=8, mantissa_bits=7)
    lo = rest - mid
    parts = jnp.concatenate([hi, mid, lo], axis=1).astype(jnp.bfloat16)
    sel = _one_hot(idx, size, jnp.bfloat16)
    out = lax.dot_general(
        sel, parts, (((0,), (0,)), ((), ())), preferred_element_type=jnp.float32
    )
    width = rows.shape[1]
    return out[:, :width] + out[:, width : 2 * width] + out[:, 2 * width :]


def _softmax_kernel(x_ref, p_ref, h_ref):
    x = x_ref[...]
    e = jnp.exp(x - jnp.max(x, axis=-1, keepdims=True))
    p = e * (1.0 / jnp.sum(e, axis=-1, keepdims=True))
    p_ref[...] = p
    half = p.astype(jnp.bfloat16)
    width = h_ref.shape[-1]
    for h in range(h_ref.shape[0]):
        h_ref[h] = half[:, h * width : (h + 1) * width]


def _softmax(logits, block_size):
    rows, width = logits.shape
    halves = width // block_size
    step = min(rows, 512)
    return pl.pallas_call(
        _softmax_kernel,
        grid=(rows // step,),
        in_specs=[pl.BlockSpec((step, width), lambda i: (i, 0))],
        out_specs=[
            pl.BlockSpec((step, width), lambda i: (i, 0)),
            pl.BlockSpec((halves, step, block_size), lambda i: (0, i, 0)),
        ],
        out_shape=[
            jax.ShapeDtypeStruct((rows, width), jnp.float32),
            jax.ShapeDtypeStruct((halves, rows, block_size), jnp.bfloat16),
        ],
        cost_estimate=pl.CostEstimate(
            flops=5 * rows * width, transcendentals=rows * width, bytes_accessed=10 * rows * width
        ),
    )(logits)


def shards(logits, tile_values, tile_pattern, tile_edge, tile_counts, capacity):
    groups = lax.axis_size("nets")
    tile_block = tile_values[0, 0]
    tile_count = tile_block.shape[0]
    block_size = tile_block.shape[1]
    slot_count = tile_count // groups
    pattern_idx = tile_pattern[0, 0]
    edge_idx = tile_edge[0, 0]
    counts = tile_counts[0, 0]
    live_slot = (jnp.arange(slot_count, dtype=jnp.int32)[None, :] < counts[:, None]).reshape(
        tile_count
    )
    weight_live = live_slot.astype(jnp.float32)
    probs, probs_split = _softmax(logits, block_size)
    segments, halves = probs_split.shape[1], probs_split.shape[0]
    probs_half = probs_split.reshape(-1, block_size)
    split_idx = lax.optimization_barrier((pattern_idx % halves) * segments + pattern_idx // halves)
    picked = _take_rows(probs_half, split_idx)
    contrib = (
        jnp.einsum("tq,tqe->te", picked, tile_block, preferred_element_type=jnp.float32)
        * weight_live[:, None]
    )
    capacity_f = capacity.reshape(-1, block_size).astype(jnp.float32)
    owned_blocks = capacity_f.shape[0]
    idx_rows = -(-slot_count // block_size)
    rows_out = -(-(slot_count + idx_rows) // 8) * 8
    edge_f = jnp.zeros((groups, idx_rows * block_size), jnp.float32).at[:, :slot_count].set(
        edge_idx.reshape(groups, slot_count).astype(jnp.float32)
    )
    payload = jnp.concatenate(
        [
            contrib.reshape(groups, slot_count, block_size),
            edge_f.reshape(groups, idx_rows, block_size),
            jnp.zeros((groups, rows_out - slot_count - idx_rows, block_size), jnp.float32),
        ],
        axis=1,
    )
    received = lax.all_to_all(payload, "nets", 0, 0, tiled=False)
    asked = (
        received[:, slot_count : slot_count + idx_rows]
        .reshape(groups, -1)[:, :slot_count]
        .astype(jnp.int32)
        .reshape(-1)
    )
    usage_edges = _add_rows(
        asked, received[:, :slot_count].reshape(-1, block_size), owned_blocks
    )
    edge_grad = jax.nn.sigmoid(usage_edges - capacity_f).astype(jnp.bfloat16)
    answer = _take_rows(edge_grad, asked).reshape(groups, slot_count, block_size)
    slot_grads = lax.all_to_all(answer, "nets", 0, 0, tiled=False).reshape(-1, block_size)
    dp_tiles = (
        jnp.einsum("tqe,te->tq", tile_block, slot_grads, preferred_element_type=jnp.float32)
        * weight_live[:, None]
    )
    idx_rows = -(-tile_count // block_size)
    idx_f = jnp.zeros((idx_rows * block_size,), jnp.float32).at[:tile_count].set(
        split_idx.astype(jnp.float32)
    )
    packed = jnp.concatenate([dp_tiles, idx_f.reshape(idx_rows, block_size)], axis=0)
    gathered = lax.all_gather(packed, "region", axis=0, tiled=False)
    all_dp = gathered[:, :tile_count].reshape(-1, block_size)
    all_idx = (
        gathered[:, tile_count:].reshape(gathered.shape[0], -1)[:, :tile_count]
        .astype(jnp.int32)
        .reshape(-1)
    )
    summed = _add_rows(all_idx, all_dp, probs_half.shape[0]).reshape(halves, segments, block_size)
    summed_grad = jnp.concatenate([summed[h] for h in range(halves)], axis=1)
    logit_grad = probs * (summed_grad - jnp.sum(probs * summed_grad, axis=-1, keepdims=True))
    return (logit_grad, usage_edges.reshape(capacity.shape))


def solution(mesh):
    in_specs = (
        P("nets", None),
        P("nets", "region", None, None, None),
        P("nets", "region", None),
        P("nets", "region", None),
        P("nets", "region", None),
        P("region", "nets"),
    )
    out_specs = (P("nets", None), P("region", "nets"))
    return jax.shard_map(shards, mesh=mesh, in_specs=in_specs, out_specs=out_specs, check_vma=False)
```

```python
import jax
import jax.numpy as jnp
from jax import lax
from jax.experimental import pallas as pl
from jax.sharding import PartitionSpec as P


def _one_hot(idx, size, dtype):
    return (idx[:, None] == jnp.arange(size, dtype=jnp.int32)[None, :]).astype(dtype)


def _take_rows(table, idx):
    sel = _one_hot(idx, table.shape[0], table.dtype)
    return jnp.dot(sel, table, preferred_element_type=jnp.float32).astype(table.dtype)


def _add_rows(idx, rows, size):
    hi = lax.reduce_precision(rows, exponent_bits=8, mantissa_bits=7)
    rest = rows - hi
    mid = lax.reduce_precision(rest, exponent_bits=8, mantissa_bits=7)
    lo = rest - mid
    parts = jnp.concatenate([hi, mid, lo], axis=1).astype(jnp.bfloat16)
    sel = _one_hot(idx, size, jnp.bfloat16)
    out = lax.dot_general(
        sel, parts, (((0,), (0,)), ((), ())), preferred_element_type=jnp.float32
    )
    width = rows.shape[1]
    return out[:, :width] + out[:, width : 2 * width] + out[:, 2 * width :]


def _softmax_kernel(x_ref, p_ref, h_ref):
    x = x_ref[...]
    e = jnp.exp(x - jnp.max(x, axis=-1, keepdims=True))
    p = e * (1.0 / jnp.sum(e, axis=-1, keepdims=True))
    p_ref[...] = p
    half = p.astype(jnp.bfloat16)
    width = h_ref.shape[-1]
    for h in range(h_ref.shape[0]):
        h_ref[h] = half[:, h * width : (h + 1) * width]


def _softmax(logits, block_size):
    rows, width = logits.shape
    halves = width // block_size
    step = min(rows, 512)
    return pl.pallas_call(
        _softmax_kernel,
        grid=(rows // step,),
        in_specs=[pl.BlockSpec((step, width), lambda i: (i, 0))],
        out_specs=[
            pl.BlockSpec((step, width), lambda i: (i, 0)),
            pl.BlockSpec((halves, step, block_size), lambda i: (0, i, 0)),
        ],
        out_shape=[
            jax.ShapeDtypeStruct((rows, width), jnp.float32),
            jax.ShapeDtypeStruct((halves, rows, block_size), jnp.bfloat16),
        ],
        cost_estimate=pl.CostEstimate(
            flops=5 * rows * width, transcendentals=rows * width, bytes_accessed=10 * rows * width
        ),
    )(logits)


def shards(logits, tile_values, tile_pattern, tile_edge, tile_counts, capacity):
    groups = lax.axis_size("nets")
    tile_block = tile_values[0, 0]
    tile_count = tile_block.shape[0]
    block_size = tile_block.shape[1]
    slot_count = tile_count // groups
    index_args = lax.optimization_barrier(
        jnp.concatenate([tile_pattern.reshape(-1), tile_edge.reshape(-1), tile_counts.reshape(-1)])
    )
    pattern_idx = index_args[:tile_count]
    edge_idx = index_args[tile_count : 2 * tile_count]
    counts = index_args[2 * tile_count :]
    live_slot = (jnp.arange(slot_count, dtype=jnp.int32)[None, :] < counts[:, None]).reshape(
        tile_count
    )
    weight_live = live_slot.astype(jnp.float32)
    probs, probs_split = _softmax(logits, block_size)
    segments, halves = probs_split.shape[1], probs_split.shape[0]
    probs_half = probs_split.reshape(-1, block_size)
    split_idx = lax.optimization_barrier((pattern_idx % halves) * segments + pattern_idx // halves)
    picked = _take_rows(probs_half, split_idx)
    contrib = (
        jnp.einsum("tq,tqe->te", picked, tile_block, preferred_element_type=jnp.float32)
        * weight_live[:, None]
    )
    capacity_f = capacity.reshape(-1, block_size).astype(jnp.float32)
    owned_blocks = capacity_f.shape[0]
    owner_idx = jnp.arange(tile_count, dtype=jnp.int32) // slot_count
    target = owner_idx * owned_blocks + edge_idx
    partial_value = _add_rows(target, contrib, groups * owned_blocks)
    received = lax.all_to_all(
        partial_value.reshape(groups, owned_blocks, block_size), "nets", 0, 0, tiled=False
    )
    usage_edges = jnp.sum(received, axis=0)
    edge_grad = jax.nn.sigmoid(usage_edges - capacity_f).astype(jnp.bfloat16)
    spread = jnp.broadcast_to(edge_grad[None], (groups, owned_blocks, block_size))
    all_grads = lax.all_to_all(spread, "nets", 0, 0, tiled=False).reshape(-1, block_size)
    slot_grads = _take_rows(all_grads, target)
    dp_tiles = (
        jnp.einsum("tqe,te->tq", tile_block, slot_grads, preferred_element_type=jnp.float32)
        * weight_live[:, None]
    )
    idx_rows = -(-tile_count // block_size)
    idx_f = jnp.zeros((idx_rows * block_size,), jnp.float32).at[:tile_count].set(
        split_idx.astype(jnp.float32)
    )
    packed = jnp.concatenate([dp_tiles, idx_f.reshape(idx_rows, block_size)], axis=0)
    gathered = lax.all_gather(packed, "region", axis=0, tiled=False)
    all_dp = gathered[:, :tile_count].reshape(-1, block_size)
    all_idx = (
        gathered[:, tile_count:].reshape(gathered.shape[0], -1)[:, :tile_count]
        .astype(jnp.int32)
        .reshape(-1)
    )
    summed = _add_rows(all_idx, all_dp, probs_half.shape[0]).reshape(halves, segments, block_size)
    summed_grad = jnp.concatenate([summed[h] for h in range(halves)], axis=1)
    logit_grad = probs * (summed_grad - jnp.sum(probs * summed_grad, axis=-1, keepdims=True))
    return (logit_grad, usage_edges.reshape(capacity.shape))


def solution(mesh):
    in_specs = (
        P("nets", None),
        P("nets", "region", None, None, None),
        P("nets", "region", None),
        P("nets", "region", None),
        P("nets", "region", None),
        P("region", "nets"),
    )
    out_specs = (P("nets", None), P("region", "nets"))
    return jax.shard_map(shards, mesh=mesh, in_specs=in_specs, out_specs=out_specs, check_vma=False)
```

```python
import jax
import jax.numpy as jnp
from jax import lax
from jax.experimental import pallas as pl
from jax.sharding import PartitionSpec as P


def _one_hot_t(idx_row, size, dtype):
    return (jnp.arange(size, dtype=jnp.int32)[:, None] == idx_row).astype(dtype)


def _take_rows(table, idx_row):
    sel = _one_hot_t(idx_row, table.shape[0], table.dtype)
    out = lax.dot_general(sel, table, (((0,), (0,)), ((), ())), preferred_element_type=jnp.float32)
    return out.astype(table.dtype)


def _add_rows(idx_row, rows, size):
    hi = lax.reduce_precision(rows, exponent_bits=8, mantissa_bits=7)
    rest = rows - hi
    mid = lax.reduce_precision(rest, exponent_bits=8, mantissa_bits=7)
    lo = rest - mid
    parts = jnp.concatenate([hi, mid, lo], axis=1).astype(jnp.bfloat16)
    sel = _one_hot_t(idx_row, size, jnp.bfloat16)
    out = jnp.dot(sel, parts, preferred_element_type=jnp.float32)
    width = rows.shape[1]
    return out[:, :width] + out[:, width : 2 * width] + out[:, 2 * width :]


def _softmax_kernel(x_ref, p_ref, h_ref):
    x = x_ref[...]
    e = jnp.exp(x - jnp.max(x, axis=-1, keepdims=True))
    p = e * (1.0 / jnp.sum(e, axis=-1, keepdims=True))
    p_ref[...] = p
    half = p.astype(jnp.bfloat16)
    width = h_ref.shape[-1]
    for h in range(h_ref.shape[0]):
        h_ref[h] = half[:, h * width : (h + 1) * width]


def _softmax(logits, block_size):
    rows, width = logits.shape
    halves = width // block_size
    step = min(rows, 512)
    return pl.pallas_call(
        _softmax_kernel,
        grid=(rows // step,),
        in_specs=[pl.BlockSpec((step, width), lambda i: (i, 0))],
        out_specs=[
            pl.BlockSpec((step, width), lambda i: (i, 0)),
            pl.BlockSpec((halves, step, block_size), lambda i: (0, i, 0)),
        ],
        out_shape=[
            jax.ShapeDtypeStruct((rows, width), jnp.float32),
            jax.ShapeDtypeStruct((halves, rows, block_size), jnp.bfloat16),
        ],
        cost_estimate=pl.CostEstimate(
            flops=5 * rows * width, transcendentals=rows * width, bytes_accessed=10 * rows * width
        ),
    )(logits)


def shards(logits, tile_values, tile_pattern, tile_edge, tile_counts, capacity):
    groups = lax.axis_size("nets")
    tile_block = tile_values[0, 0]
    tile_count = tile_block.shape[0]
    block_size = tile_block.shape[1]
    slot_count = tile_count // groups
    pattern_idx = tile_pattern[0]
    edge_idx = tile_edge[0]
    counts = tile_counts[0]
    slot = jnp.arange(tile_count, dtype=jnp.int32)[None, :]
    owner_idx = slot // slot_count
    slot_limit = jnp.sum(
        jnp.where(owner_idx == jnp.arange(groups, dtype=jnp.int32)[:, None], counts.T, 0),
        axis=0,
        keepdims=True,
    )
    live = slot % slot_count < slot_limit
    probs, probs_split = _softmax(logits, block_size)
    segments, halves = probs_split.shape[1], probs_split.shape[0]
    probs_half = probs_split.reshape(-1, block_size)
    split_idx = (pattern_idx % halves) * segments + pattern_idx // halves
    picked = _take_rows(probs_half, split_idx)
    contrib = jnp.einsum("tq,tqe->te", picked, tile_block, preferred_element_type=jnp.float32)
    capacity_f = capacity.reshape(-1, block_size).astype(jnp.float32)
    owned_blocks = capacity_f.shape[0]
    target = owner_idx * owned_blocks + edge_idx
    partial_value = _add_rows(jnp.where(live, target, -1), contrib, groups * owned_blocks)
    received = lax.all_to_all(
        partial_value.reshape(groups, owned_blocks, block_size), "nets", 0, 0, tiled=False
    )
    usage_edges = jnp.sum(received, axis=0)
    edge_grad = jax.nn.sigmoid(usage_edges - capacity_f).astype(jnp.bfloat16)
    spread = jnp.broadcast_to(edge_grad[None], (groups, owned_blocks, block_size))
    all_grads = lax.all_to_all(spread, "nets", 0, 0, tiled=False).reshape(-1, block_size)
    slot_grads = _take_rows(all_grads, target)
    dp_tiles = jnp.einsum("tqe,te->tq", tile_block, slot_grads, preferred_element_type=jnp.float32)
    idx_rows = -(-tile_count // block_size)
    idx_f = jnp.full((1, idx_rows * block_size), -1.0, jnp.float32).at[:, :tile_count].set(
        jnp.where(live, split_idx, -1).astype(jnp.float32)
    )
    packed = jnp.concatenate([dp_tiles, idx_f.reshape(idx_rows, block_size)], axis=0)
    gathered = lax.all_gather(packed, "region", axis=0, tiled=False)
    all_dp = gathered[:, :tile_count].reshape(-1, block_size)
    all_idx = (
        gathered[:, tile_count:].reshape(gathered.shape[0], -1)[:, :tile_count]
        .astype(jnp.int32)
        .reshape(1, -1)
    )
    summed = _add_rows(all_idx, all_dp, probs_half.shape[0]).reshape(halves, segments, block_size)
    summed_grad = jnp.concatenate([summed[h] for h in range(halves)], axis=1)
    logit_grad = probs * (summed_grad - jnp.sum(probs * summed_grad, axis=-1, keepdims=True))
    return (logit_grad, usage_edges.reshape(capacity.shape))


def solution(mesh):
    in_specs = (
        P("nets", None),
        P("nets", "region", None, None, None),
        P("nets", "region", None),
        P("nets", "region", None),
        P("nets", "region", None),
        P("region", "nets"),
    )
    out_specs = (P("nets", None), P("region", "nets"))
    return jax.shard_map(shards, mesh=mesh, in_specs=in_specs, out_specs=out_specs, check_vma=False)
```

```python
import jax
import jax.numpy as jnp
from jax import lax
from jax.experimental import pallas as pl
from jax.sharding import PartitionSpec as P


def _one_hot_t(idx_row, size, dtype):
    return (jnp.arange(size, dtype=jnp.int32)[:, None] == idx_row).astype(dtype)


def _take_rows(table, idx_row):
    sel = _one_hot_t(idx_row, table.shape[0], table.dtype)
    out = lax.dot_general(sel, table, (((0,), (0,)), ((), ())), preferred_element_type=jnp.float32)
    return out.astype(table.dtype)


def _add_rows(idx_row, rows, size):
    hi = lax.reduce_precision(rows, exponent_bits=8, mantissa_bits=7)
    rest = rows - hi
    mid = lax.reduce_precision(rest, exponent_bits=8, mantissa_bits=7)
    lo = rest - mid
    parts = jnp.concatenate([hi, mid, lo], axis=1).astype(jnp.bfloat16)
    sel = _one_hot_t(idx_row, size, jnp.bfloat16)
    out = jnp.dot(sel, parts, preferred_element_type=jnp.float32)
    width = rows.shape[1]
    return out[:, :width] + out[:, width : 2 * width] + out[:, 2 * width :]


def _softmax_kernel(x_ref, idx_ref, p_ref, pick_ref):
    x = x_ref[...]
    e = jnp.exp(x - jnp.max(x, axis=-1, keepdims=True))
    p = e * (1.0 / jnp.sum(e, axis=-1, keepdims=True))
    p_ref[...] = p
    half = p.astype(jnp.bfloat16)
    rows, width = half.shape
    block_size = pick_ref.shape[-1]
    halves = width // block_size
    idx = idx_ref[...]
    seg = lax.broadcasted_iota(jnp.int32, (1, rows), 1) * halves
    picked = None
    for h in range(halves):
        sel = (idx == seg + h).astype(jnp.bfloat16)
        part = jnp.dot(
            sel, half[:, h * block_size : (h + 1) * block_size], preferred_element_type=jnp.float32
        )
        picked = part if picked is None else picked + part
    pick_ref[...] = picked.astype(jnp.bfloat16)


def _softmax(logits, idx_col, block_size):
    rows, width = logits.shape
    tiles = idx_col.shape[0]
    return pl.pallas_call(
        _softmax_kernel,
        out_shape=[
            jax.ShapeDtypeStruct((rows, width), jnp.float32),
            jax.ShapeDtypeStruct((tiles, block_size), jnp.bfloat16),
        ],
        cost_estimate=pl.CostEstimate(
            flops=5 * rows * width + 2 * tiles * rows * width,
            transcendentals=rows * width,
            bytes_accessed=8 * rows * width + 4 * tiles + 2 * tiles * block_size,
        ),
    )(logits, idx_col)


def shards(logits, tile_values, tile_pattern, tile_edge, tile_counts, capacity):
    groups = lax.axis_size("nets")
    tile_block = tile_values[0, 0]
    tile_count = tile_block.shape[0]
    block_size = tile_block.shape[1]
    slot_count = tile_count // groups
    pattern_idx = tile_pattern[0]
    edge_idx = tile_edge[0]
    counts = tile_counts[0]
    slot = jnp.arange(tile_count, dtype=jnp.int32)[None, :]
    owner_idx = slot // slot_count
    slot_limit = jnp.sum(
        jnp.where(owner_idx == jnp.arange(groups, dtype=jnp.int32)[:, None], counts.T, 0),
        axis=0,
        keepdims=True,
    )
    live = slot % slot_count < slot_limit
    probs, picked = _softmax(logits, tile_pattern.reshape(tile_count, 1), block_size)
    segments, halves = logits.shape[0], logits.shape[1] // block_size
    split_idx = (pattern_idx % halves) * segments + pattern_idx // halves
    contrib = jnp.einsum("tq,tqe->te", picked, tile_block, preferred_element_type=jnp.float32)
    capacity_f = capacity.reshape(-1, block_size).astype(jnp.float32)
    owned_blocks = capacity_f.shape[0]
    target = owner_idx * owned_blocks + edge_idx
    partial_value = _add_rows(jnp.where(live, target, -1), contrib, groups * owned_blocks)
    received = lax.all_to_all(
        partial_value.reshape(groups, owned_blocks, block_size), "nets", 0, 0, tiled=False
    )
    usage_edges = jnp.sum(received, axis=0)
    edge_grad = jax.nn.sigmoid(usage_edges - capacity_f).astype(jnp.bfloat16)
    spread = jnp.broadcast_to(edge_grad[None], (groups, owned_blocks, block_size))
    all_grads = lax.all_to_all(spread, "nets", 0, 0, tiled=False).reshape(-1, block_size)
    slot_grads = _take_rows(all_grads, target)
    dp_tiles = jnp.einsum("tqe,te->tq", tile_block, slot_grads, preferred_element_type=jnp.float32)
    idx_rows = -(-tile_count // block_size)
    idx_f = jnp.full((1, idx_rows * block_size), -1.0, jnp.float32).at[:, :tile_count].set(
        jnp.where(live, split_idx, -1).astype(jnp.float32)
    )
    packed = jnp.concatenate([dp_tiles, idx_f.reshape(idx_rows, block_size)], axis=0)
    gathered = lax.all_gather(packed, "region", axis=0, tiled=False)
    all_dp = gathered[:, :tile_count].reshape(-1, block_size)
    all_idx = (
        gathered[:, tile_count:].reshape(gathered.shape[0], -1)[:, :tile_count]
        .astype(jnp.int32)
        .reshape(1, -1)
    )
    summed = _add_rows(all_idx, all_dp, halves * segments).reshape(halves, segments, block_size)
    summed_grad = jnp.concatenate([summed[h] for h in range(halves)], axis=1)
    logit_grad = probs * (summed_grad - jnp.sum(probs * summed_grad, axis=-1, keepdims=True))
    return (logit_grad, usage_edges.reshape(capacity.shape))


def solution(mesh):
    in_specs = (
        P("nets", None),
        P("nets", "region", None, None, None),
        P("nets", "region", None),
        P("nets", "region", None),
        P("nets", "region", None),
        P("region", "nets"),
    )
    out_specs = (P("nets", None), P("region", "nets"))
    return jax.shard_map(shards, mesh=mesh, in_specs=in_specs, out_specs=out_specs, check_vma=False)
```

```python
import jax
import jax.numpy as jnp
from jax import lax
from jax.experimental import pallas as pl
from jax.sharding import PartitionSpec as P


def _one_hot_t(idx_row, size, dtype):
    return (jnp.arange(size, dtype=jnp.int32)[:, None] == idx_row).astype(dtype)


def _take_rows(table, idx_row):
    sel = _one_hot_t(idx_row, table.shape[0], table.dtype)
    out = lax.dot_general(sel, table, (((0,), (0,)), ((), ())), preferred_element_type=jnp.float32)
    return out.astype(table.dtype)


def _add_rows(idx_row, rows, size):
    hi = lax.reduce_precision(rows, exponent_bits=8, mantissa_bits=7)
    rest = rows - hi
    mid = lax.reduce_precision(rest, exponent_bits=8, mantissa_bits=7)
    lo = rest - mid
    parts = jnp.concatenate([hi, mid, lo], axis=0).astype(jnp.bfloat16)
    sel = _one_hot_t(jnp.concatenate([idx_row] * 3, axis=1), size, jnp.bfloat16)
    return jnp.dot(sel, parts, preferred_element_type=jnp.float32)


def _softmax_kernel(x_ref, p_ref, h_ref):
    x = x_ref[...]
    e = jnp.exp(x - jnp.max(x, axis=-1, keepdims=True))
    p = e * (1.0 / jnp.sum(e, axis=-1, keepdims=True))
    p_ref[...] = p
    half = p.astype(jnp.bfloat16)
    width = h_ref.shape[-1]
    for h in range(h_ref.shape[0]):
        h_ref[h] = half[:, h * width : (h + 1) * width]


def _softmax(logits, block_size):
    rows, width = logits.shape
    halves = width // block_size
    step = min(rows, 512)
    return pl.pallas_call(
        _softmax_kernel,
        grid=(rows // step,),
        in_specs=[pl.BlockSpec((step, width), lambda i: (i, 0))],
        out_specs=[
            pl.BlockSpec((step, width), lambda i: (i, 0)),
            pl.BlockSpec((halves, step, block_size), lambda i: (0, i, 0)),
        ],
        out_shape=[
            jax.ShapeDtypeStruct((rows, width), jnp.float32),
            jax.ShapeDtypeStruct((halves, rows, block_size), jnp.bfloat16),
        ],
        cost_estimate=pl.CostEstimate(
            flops=5 * rows * width, transcendentals=rows * width, bytes_accessed=10 * rows * width
        ),
    )(logits)


def shards(logits, tile_values, tile_pattern, tile_edge, tile_counts, capacity):
    groups = lax.axis_size("nets")
    tile_block = tile_values[0, 0]
    tile_count = tile_block.shape[0]
    block_size = tile_block.shape[1]
    slot_count = tile_count // groups
    pattern_idx = tile_pattern[0]
    edge_idx = tile_edge[0]
    counts = tile_counts[0]
    slot = jnp.arange(tile_count, dtype=jnp.int32)[None, :]
    owner_idx = slot // slot_count
    slot_limit = jnp.sum(
        jnp.where(owner_idx == jnp.arange(groups, dtype=jnp.int32)[:, None], counts.T, 0),
        axis=0,
        keepdims=True,
    )
    live = slot % slot_count < slot_limit
    probs, probs_split = _softmax(logits, block_size)
    segments, halves = probs_split.shape[1], probs_split.shape[0]
    probs_half = probs_split.reshape(-1, block_size)
    split_idx = (pattern_idx % halves) * segments + pattern_idx // halves
    picked = _take_rows(probs_half, split_idx)
    contrib = jnp.einsum("tq,tqe->te", picked, tile_block, preferred_element_type=jnp.float32)
    capacity_f = capacity.reshape(-1, block_size).astype(jnp.float32)
    owned_blocks = capacity_f.shape[0]
    target = owner_idx * owned_blocks + edge_idx
    partial_value = _add_rows(jnp.where(live, target, -1), contrib, groups * owned_blocks)
    received = lax.all_to_all(
        partial_value.reshape(groups, owned_blocks, block_size), "nets", 0, 0, tiled=False
    )
    usage_edges = jnp.sum(received, axis=0)
    edge_grad = jax.nn.sigmoid(usage_edges - capacity_f).astype(jnp.bfloat16)
    spread = jnp.broadcast_to(edge_grad[None], (groups, owned_blocks, block_size))
    all_grads = lax.all_to_all(spread, "nets", 0, 0, tiled=False).reshape(-1, block_size)
    slot_grads = _take_rows(all_grads, target)
    dp_tiles = jnp.einsum("tqe,te->tq", tile_block, slot_grads, preferred_element_type=jnp.float32)
    idx_rows = -(-tile_count // block_size)
    idx_f = jnp.full((1, idx_rows * block_size), -1.0, jnp.float32).at[:, :tile_count].set(
        jnp.where(live, split_idx, -1).astype(jnp.float32)
    )
    packed = jnp.concatenate([dp_tiles, idx_f.reshape(idx_rows, block_size)], axis=0)
    gathered = lax.all_gather(packed, "region", axis=0, tiled=False)
    all_dp = gathered[:, :tile_count].reshape(-1, block_size)
    all_idx = (
        gathered[:, tile_count:].reshape(gathered.shape[0], -1)[:, :tile_count]
        .astype(jnp.int32)
        .reshape(1, -1)
    )
    summed = _add_rows(all_idx, all_dp, probs_half.shape[0]).reshape(halves, segments, block_size)
    summed_grad = jnp.concatenate([summed[h] for h in range(halves)], axis=1)
    logit_grad = probs * (summed_grad - jnp.sum(probs * summed_grad, axis=-1, keepdims=True))
    return (logit_grad, usage_edges.reshape(capacity.shape))


def solution(mesh):
    in_specs = (
        P("nets", None),
        P("nets", "region", None, None, None),
        P("nets", "region", None),
        P("nets", "region", None),
        P("nets", "region", None),
        P("region", "nets"),
    )
    out_specs = (P("nets", None), P("region", "nets"))
    return jax.shard_map(shards, mesh=mesh, in_specs=in_specs, out_specs=out_specs, check_vma=False)
```

```python
import jax
import jax.numpy as jnp
from jax import lax
from jax.experimental import pallas as pl
from jax.sharding import PartitionSpec as P


def _one_hot_t(idx_row, size, dtype):
    return (jnp.arange(size, dtype=jnp.int32)[:, None] == idx_row).astype(dtype)


def _take_rows(table, idx_row):
    sel = _one_hot_t(idx_row, table.shape[0], table.dtype)
    out = lax.dot_general(sel, table, (((0,), (0,)), ((), ())), preferred_element_type=jnp.float32)
    return out.astype(table.dtype)


def _add_rows(idx_row, rows, size):
    hi = lax.reduce_precision(rows, exponent_bits=8, mantissa_bits=7)
    rest = rows - hi
    mid = lax.reduce_precision(rest, exponent_bits=8, mantissa_bits=7)
    lo = rest - mid
    parts = jnp.concatenate([hi, mid, lo], axis=1).astype(jnp.bfloat16)
    sel = _one_hot_t(idx_row, size, jnp.bfloat16)
    out = jnp.dot(sel, parts, preferred_element_type=jnp.float32)
    width = rows.shape[1]
    return out[:, :width] + out[:, width : 2 * width] + out[:, 2 * width :]


def _softmax_kernel(x_ref, p_ref, h_ref):
    x = x_ref[...]
    e = jnp.exp(x - jnp.max(x, axis=-1, keepdims=True))
    p = e * (1.0 / jnp.sum(e, axis=-1, keepdims=True))
    p_ref[...] = p
    half = p.astype(jnp.bfloat16)
    width = h_ref.shape[-1]
    for h in range(h_ref.shape[0]):
        h_ref[h] = half[:, h * width : (h + 1) * width]


def _softmax(logits, block_size):
    rows, width = logits.shape
    halves = width // block_size
    step = min(rows, 512)
    return pl.pallas_call(
        _softmax_kernel,
        grid=(rows // step,),
        in_specs=[pl.BlockSpec((step, width), lambda i: (i, 0))],
        out_specs=[
            pl.BlockSpec((step, width), lambda i: (i, 0)),
            pl.BlockSpec((halves, step, block_size), lambda i: (0, i, 0)),
        ],
        out_shape=[
            jax.ShapeDtypeStruct((rows, width), jnp.float32),
            jax.ShapeDtypeStruct((halves, rows, block_size), jnp.bfloat16),
        ],
        cost_estimate=pl.CostEstimate(
            flops=5 * rows * width, transcendentals=rows * width, bytes_accessed=10 * rows * width
        ),
    )(logits)


def _vjp_kernel(p_ref, g_ref, o_ref):
    p = p_ref[...]
    block_size = g_ref.shape[-1]
    halves = g_ref.shape[0]
    cols = [slice(h * block_size, (h + 1) * block_size) for h in range(halves)]
    dot = sum(jnp.sum(p[:, c] * g_ref[h], axis=-1, keepdims=True) for h, c in enumerate(cols))
    for h, c in enumerate(cols):
        o_ref[:, c] = p[:, c] * (g_ref[h] - dot)


def _softmax_vjp(probs, grads):
    rows, width = probs.shape
    halves, _, block_size = grads.shape
    step = min(rows, 256)
    return pl.pallas_call(
        _vjp_kernel,
        grid=(rows // step,),
        in_specs=[
            pl.BlockSpec((step, width), lambda i: (i, 0)),
            pl.BlockSpec((halves, step, block_size), lambda i: (0, i, 0)),
        ],
        out_specs=pl.BlockSpec((step, width), lambda i: (i, 0)),
        out_shape=jax.ShapeDtypeStruct((rows, width), jnp.float32),
        cost_estimate=pl.CostEstimate(
            flops=4 * rows * width, transcendentals=0, bytes_accessed=12 * rows * width
        ),
    )(probs, grads)


def shards(logits, tile_values, tile_pattern, tile_edge, tile_counts, capacity):
    groups = lax.axis_size("nets")
    tile_block = tile_values[0, 0]
    tile_count = tile_block.shape[0]
    block_size = tile_block.shape[1]
    slot_count = tile_count // groups
    pattern_idx = tile_pattern[0]
    edge_idx = tile_edge[0]
    counts = tile_counts[0]
    slot = jnp.arange(tile_count, dtype=jnp.int32)[None, :]
    owner_idx = slot // slot_count
    slot_limit = jnp.sum(
        jnp.where(owner_idx == jnp.arange(groups, dtype=jnp.int32)[:, None], counts.T, 0),
        axis=0,
        keepdims=True,
    )
    live = slot % slot_count < slot_limit
    probs, probs_split = _softmax(logits, block_size)
    segments, halves = probs_split.shape[1], probs_split.shape[0]
    probs_half = probs_split.reshape(-1, block_size)
    split_idx = (pattern_idx % halves) * segments + pattern_idx // halves
    picked = _take_rows(probs_half, split_idx)
    contrib = jnp.einsum("tq,tqe->te", picked, tile_block, preferred_element_type=jnp.float32)
    capacity_f = capacity.reshape(-1, block_size).astype(jnp.float32)
    owned_blocks = capacity_f.shape[0]
    target = owner_idx * owned_blocks + edge_idx
    partial_value = _add_rows(jnp.where(live, target, -1), contrib, groups * owned_blocks)
    received = lax.all_to_all(
        partial_value.reshape(groups, owned_blocks, block_size), "nets", 0, 0, tiled=False
    )
    usage_edges = jnp.sum(received, axis=0)
    edge_grad = jax.nn.sigmoid(usage_edges - capacity_f).astype(jnp.bfloat16)
    spread = jnp.broadcast_to(edge_grad[None], (groups, owned_blocks, block_size))
    all_grads = lax.all_to_all(spread, "nets", 0, 0, tiled=False).reshape(-1, block_size)
    slot_grads = _take_rows(all_grads, target)
    dp_tiles = jnp.einsum("tqe,te->tq", tile_block, slot_grads, preferred_element_type=jnp.float32)
    idx_rows = -(-tile_count // block_size)
    idx_f = jnp.full((1, idx_rows * block_size), -1.0, jnp.float32).at[:, :tile_count].set(
        jnp.where(live, split_idx, -1).astype(jnp.float32)
    )
    packed = jnp.concatenate([dp_tiles, idx_f.reshape(idx_rows, block_size)], axis=0)
    gathered = lax.all_gather(packed, "region", axis=0, tiled=False)
    all_dp = gathered[:, :tile_count].reshape(-1, block_size)
    all_idx = (
        gathered[:, tile_count:].reshape(gathered.shape[0], -1)[:, :tile_count]
        .astype(jnp.int32)
        .reshape(1, -1)
    )
    summed = _add_rows(all_idx, all_dp, probs_half.shape[0]).reshape(halves, segments, block_size)
    logit_grad = _softmax_vjp(probs, summed)
    return (logit_grad, usage_edges.reshape(capacity.shape))


def solution(mesh):
    in_specs = (
        P("nets", None),
        P("nets", "region", None, None, None),
        P("nets", "region", None),
        P("nets", "region", None),
        P("nets", "region", None),
        P("region", "nets"),
    )
    out_specs = (P("nets", None), P("region", "nets"))
    return jax.shard_map(shards, mesh=mesh, in_specs=in_specs, out_specs=out_specs, check_vma=False)
```

```python
import jax
import jax.numpy as jnp
from jax import lax
from jax.experimental import pallas as pl
from jax.sharding import PartitionSpec as P


def _one_hot_t(idx_row, size, dtype):
    return (jnp.arange(size, dtype=jnp.int32)[:, None] == idx_row).astype(dtype)


def _take_rows(table, idx_row):
    sel = _one_hot_t(idx_row, table.shape[0], table.dtype)
    out = lax.dot_general(sel, table, (((0,), (0,)), ((), ())), preferred_element_type=jnp.float32)
    return out.astype(table.dtype)


def _add_rows(idx_row, rows, size):
    hi = lax.reduce_precision(rows, exponent_bits=8, mantissa_bits=7)
    rest = rows - hi
    mid = lax.reduce_precision(rest, exponent_bits=8, mantissa_bits=7)
    lo = rest - mid
    parts = jnp.concatenate([hi, mid, lo], axis=1).astype(jnp.bfloat16)
    sel = _one_hot_t(idx_row, size, jnp.bfloat16)
    out = jnp.dot(sel, parts, preferred_element_type=jnp.float32)
    width = rows.shape[1]
    return out[:, :width] + out[:, width : 2 * width] + out[:, 2 * width :]


def _softmax_kernel(x_ref, p_ref, h_ref):
    x = x_ref[...]
    e = jnp.exp(x - jnp.max(x, axis=-1, keepdims=True))
    p = e * (1.0 / jnp.sum(e, axis=-1, keepdims=True))
    p_ref[...] = p
    half = p.astype(jnp.bfloat16)
    width = h_ref.shape[-1]
    for h in range(h_ref.shape[0]):
        h_ref[h] = half[:, h * width : (h + 1) * width]


def _softmax(logits, block_size):
    rows, width = logits.shape
    halves = width // block_size
    step = min(rows, 512)
    return pl.pallas_call(
        _softmax_kernel,
        grid=(rows // step,),
        in_specs=[pl.BlockSpec((step, width), lambda i: (i, 0))],
        out_specs=[
            pl.BlockSpec((step, width), lambda i: (i, 0)),
            pl.BlockSpec((halves, step, block_size), lambda i: (0, i, 0)),
        ],
        out_shape=[
            jax.ShapeDtypeStruct((rows, width), jnp.float32),
            jax.ShapeDtypeStruct((halves, rows, block_size), jnp.bfloat16),
        ],
        cost_estimate=pl.CostEstimate(
            flops=5 * rows * width, transcendentals=rows * width, bytes_accessed=10 * rows * width
        ),
    )(logits)


def shards(logits, tile_values, tile_pattern, tile_edge, tile_counts, capacity):
    groups = lax.axis_size("nets")
    tile_block = tile_values[0, 0]
    tile_count = tile_block.shape[0]
    block_size = tile_block.shape[1]
    slot_count = tile_count // groups
    pattern_idx = tile_pattern[0]
    edge_idx = tile_edge[0]
    counts = tile_counts[0]
    slot = jnp.arange(tile_count, dtype=jnp.int32)[None, :]
    owner_idx = slot // slot_count
    slot_limit = jnp.sum(
        jnp.where(owner_idx == jnp.arange(groups, dtype=jnp.int32)[:, None], counts.T, 0),
        axis=0,
        keepdims=True,
    )
    live = slot % slot_count < slot_limit
    probs, probs_split = _softmax(logits, block_size)
    segments, halves = probs_split.shape[1], probs_split.shape[0]
    probs_half = probs_split.reshape(-1, block_size)
    split_idx = (pattern_idx % halves) * segments + pattern_idx // halves
    picked = jnp.take(probs_half, split_idx[0], axis=0, mode="clip")
    contrib = jnp.einsum("tq,tqe->te", picked, tile_block, preferred_element_type=jnp.float32)
    capacity_f = capacity.reshape(-1, block_size).astype(jnp.float32)
    owned_blocks = capacity_f.shape[0]
    target = owner_idx * owned_blocks + edge_idx
    partial_value = _add_rows(jnp.where(live, target, -1), contrib, groups * owned_blocks)
    received = lax.all_to_all(
        partial_value.reshape(groups, owned_blocks, block_size), "nets", 0, 0, tiled=False
    )
    usage_edges = jnp.sum(received, axis=0)
    edge_grad = jax.nn.sigmoid(usage_edges - capacity_f).astype(jnp.bfloat16)
    spread = jnp.broadcast_to(edge_grad[None], (groups, owned_blocks, block_size))
    all_grads = lax.all_to_all(spread, "nets", 0, 0, tiled=False).reshape(-1, block_size)
    slot_grads = _take_rows(all_grads, target)
    dp_tiles = jnp.einsum("tqe,te->tq", tile_block, slot_grads, preferred_element_type=jnp.float32)
    idx_rows = -(-tile_count // block_size)
    idx_f = jnp.full((1, idx_rows * block_size), -1.0, jnp.float32).at[:, :tile_count].set(
        jnp.where(live, split_idx, -1).astype(jnp.float32)
    )
    packed = jnp.concatenate([dp_tiles, idx_f.reshape(idx_rows, block_size)], axis=0)
    gathered = lax.all_gather(packed, "region", axis=0, tiled=False)
    all_dp = gathered[:, :tile_count].reshape(-1, block_size)
    all_idx = (
        gathered[:, tile_count:].reshape(gathered.shape[0], -1)[:, :tile_count]
        .astype(jnp.int32)
        .reshape(1, -1)
    )
    summed = _add_rows(all_idx, all_dp, probs_half.shape[0]).reshape(halves, segments, block_size)
    summed_grad = jnp.concatenate([summed[h] for h in range(halves)], axis=1)
    logit_grad = probs * (summed_grad - jnp.sum(probs * summed_grad, axis=-1, keepdims=True))
    return (logit_grad, usage_edges.reshape(capacity.shape))


def solution(mesh):
    in_specs = (
        P("nets", None),
        P("nets", "region", None, None, None),
        P("nets", "region", None),
        P("nets", "region", None),
        P("nets", "region", None),
        P("region", "nets"),
    )
    out_specs = (P("nets", None), P("region", "nets"))
    return jax.shard_map(shards, mesh=mesh, in_specs=in_specs, out_specs=out_specs, check_vma=False)
```

```python
import jax
import jax.numpy as jnp
from jax import lax
from jax.experimental import pallas as pl
from jax.sharding import PartitionSpec as P


def _one_hot_t(idx_row, size, dtype):
    return (jnp.arange(size, dtype=jnp.int32)[:, None] == idx_row).astype(dtype)


def _take_rows(table, idx_row):
    sel = _one_hot_t(idx_row, table.shape[0], table.dtype)
    out = lax.dot_general(sel, table, (((0,), (0,)), ((), ())), preferred_element_type=jnp.float32)
    return out.astype(table.dtype)


def _add_rows(idx_row, rows, size):
    hi = lax.reduce_precision(rows, exponent_bits=8, mantissa_bits=7)
    rest = rows - hi
    mid = lax.reduce_precision(rest, exponent_bits=8, mantissa_bits=7)
    lo = rest - mid
    parts = jnp.concatenate([hi, mid, lo], axis=1).astype(jnp.bfloat16)
    sel = _one_hot_t(idx_row, size, jnp.bfloat16)
    out = jnp.dot(sel, parts, preferred_element_type=jnp.float32)
    width = rows.shape[1]
    return out[:, :width] + out[:, width : 2 * width] + out[:, 2 * width :]


def _softmax_kernel(x_ref, p_ref, h_ref):
    x = x_ref[...]
    e = jnp.exp(x - jnp.max(x, axis=-1, keepdims=True))
    p = e * (1.0 / jnp.sum(e, axis=-1, keepdims=True))
    p_ref[...] = p
    half = p.astype(jnp.bfloat16)
    width = h_ref.shape[-1]
    for h in range(h_ref.shape[0]):
        h_ref[h] = half[:, h * width : (h + 1) * width]


def _softmax(logits, block_size):
    rows, width = logits.shape
    halves = width // block_size
    step = rows
    return pl.pallas_call(
        _softmax_kernel,
        grid=(rows // step,),
        in_specs=[pl.BlockSpec((step, width), lambda i: (i, 0))],
        out_specs=[
            pl.BlockSpec((step, width), lambda i: (i, 0)),
            pl.BlockSpec((halves, step, block_size), lambda i: (0, i, 0)),
        ],
        out_shape=[
            jax.ShapeDtypeStruct((rows, width), jnp.float32),
            jax.ShapeDtypeStruct((halves, rows, block_size), jnp.bfloat16),
        ],
        cost_estimate=pl.CostEstimate(
            flops=5 * rows * width, transcendentals=rows * width, bytes_accessed=10 * rows * width
        ),
    )(logits)


def shards(logits, tile_values, tile_pattern, tile_edge, tile_counts, capacity):
    groups = lax.axis_size("nets")
    tile_block = tile_values[0, 0]
    tile_count = tile_block.shape[0]
    block_size = tile_block.shape[1]
    slot_count = tile_count // groups
    pattern_idx = tile_pattern[0]
    edge_idx = tile_edge[0]
    counts = tile_counts[0]
    slot = jnp.arange(tile_count, dtype=jnp.int32)[None, :]
    owner_idx = slot // slot_count
    slot_limit = jnp.sum(
        jnp.where(owner_idx == jnp.arange(groups, dtype=jnp.int32)[:, None], counts.T, 0),
        axis=0,
        keepdims=True,
    )
    live = slot % slot_count < slot_limit
    probs, probs_split = _softmax(logits, block_size)
    segments, halves = probs_split.shape[1], probs_split.shape[0]
    probs_half = probs_split.reshape(-1, block_size)
    split_idx = (pattern_idx % halves) * segments + pattern_idx // halves
    picked = jnp.take(probs_half, split_idx[0], axis=0, mode="clip")
    contrib = jnp.einsum("tq,tqe->te", picked, tile_block, preferred_element_type=jnp.float32)
    capacity_f = capacity.reshape(-1, block_size).astype(jnp.float32)
    owned_blocks = capacity_f.shape[0]
    target = owner_idx * owned_blocks + edge_idx
    partial_value = _add_rows(jnp.where(live, target, -1), contrib, groups * owned_blocks)
    received = lax.all_to_all(
        partial_value.reshape(groups, owned_blocks, block_size), "nets", 0, 0, tiled=False
    )
    usage_edges = jnp.sum(received, axis=0)
    edge_grad = jax.nn.sigmoid(usage_edges - capacity_f).astype(jnp.bfloat16)
    spread = jnp.broadcast_to(edge_grad[None], (groups, owned_blocks, block_size))
    all_grads = lax.all_to_all(spread, "nets", 0, 0, tiled=False).reshape(-1, block_size)
    slot_grads = _take_rows(all_grads, target)
    dp_tiles = jnp.einsum("tqe,te->tq", tile_block, slot_grads, preferred_element_type=jnp.float32)
    idx_rows = -(-tile_count // block_size)
    idx_f = jnp.full((1, idx_rows * block_size), -1.0, jnp.float32).at[:, :tile_count].set(
        jnp.where(live, split_idx, -1).astype(jnp.float32)
    )
    packed = jnp.concatenate([dp_tiles, idx_f.reshape(idx_rows, block_size)], axis=0)
    gathered = lax.all_gather(packed, "region", axis=0, tiled=False)
    all_dp = gathered[:, :tile_count].reshape(-1, block_size)
    all_idx = (
        gathered[:, tile_count:].reshape(gathered.shape[0], -1)[:, :tile_count]
        .astype(jnp.int32)
        .reshape(1, -1)
    )
    summed = _add_rows(all_idx, all_dp, probs_half.shape[0]).reshape(halves, segments, block_size)
    summed_grad = jnp.concatenate([summed[h] for h in range(halves)], axis=1)
    logit_grad = probs * (summed_grad - jnp.sum(probs * summed_grad, axis=-1, keepdims=True))
    return (logit_grad, usage_edges.reshape(capacity.shape))


def solution(mesh):
    in_specs = (
        P("nets", None),
        P("nets", "region", None, None, None),
        P("nets", "region", None),
        P("nets", "region", None),
        P("nets", "region", None),
        P("region", "nets"),
    )
    out_specs = (P("nets", None), P("region", "nets"))
    return jax.shard_map(shards, mesh=mesh, in_specs=in_specs, out_specs=out_specs, check_vma=False)
```

```python
import jax
import jax.numpy as jnp
from jax import lax
from jax.experimental import pallas as pl
from jax.sharding import PartitionSpec as P


def _one_hot_t(idx_row, size, dtype):
    return (jnp.arange(size, dtype=jnp.int32)[:, None] == idx_row).astype(dtype)


def _take_rows(table, idx_row):
    sel = _one_hot_t(idx_row, table.shape[0], table.dtype)
    out = lax.dot_general(sel, table, (((0,), (0,)), ((), ())), preferred_element_type=jnp.float32)
    return out.astype(table.dtype)


def _add_rows(idx_row, rows, size):
    hi = lax.reduce_precision(rows, exponent_bits=8, mantissa_bits=7)
    rest = rows - hi
    mid = lax.reduce_precision(rest, exponent_bits=8, mantissa_bits=7)
    lo = rest - mid
    parts = jnp.concatenate([hi, mid, lo], axis=1).astype(jnp.bfloat16)
    sel = _one_hot_t(idx_row, size, jnp.bfloat16)
    out = jnp.dot(sel, parts, preferred_element_type=jnp.float32)
    width = rows.shape[1]
    return out[:, :width] + out[:, width : 2 * width] + out[:, 2 * width :]


def _softmax_kernel(x_ref, p_ref, h_ref):
    x = x_ref[...]
    e = jnp.exp(x - jnp.max(x, axis=-1, keepdims=True))
    p = e * (1.0 / jnp.sum(e, axis=-1, keepdims=True))
    p_ref[...] = p
    half = p.astype(jnp.bfloat16)
    width = h_ref.shape[-1]
    for h in range(h_ref.shape[0]):
        h_ref[h] = half[:, h * width : (h + 1) * width]


def _softmax(logits, block_size):
    rows, width = logits.shape
    halves = width // block_size
    step = min(rows, 512)
    return pl.pallas_call(
        _softmax_kernel,
        grid=(rows // step,),
        in_specs=[pl.BlockSpec((step, width), lambda i: (i, 0))],
        out_specs=[
            pl.BlockSpec((step, width), lambda i: (i, 0)),
            pl.BlockSpec((halves, step, block_size), lambda i: (0, i, 0)),
        ],
        out_shape=[
            jax.ShapeDtypeStruct((rows, width), jnp.float32),
            jax.ShapeDtypeStruct((halves, rows, block_size), jnp.bfloat16),
        ],
        cost_estimate=pl.CostEstimate(
            flops=5 * rows * width, transcendentals=rows * width, bytes_accessed=10 * rows * width
        ),
    )(logits)


def shards(logits, tile_values, tile_pattern, tile_edge, tile_counts, capacity):
    groups = lax.axis_size("nets")
    tile_block = tile_values[0, 0]
    tile_count = tile_block.shape[0]
    block_size = tile_block.shape[1]
    slot_count = tile_count // groups
    pattern_idx = tile_pattern[0]
    edge_idx = tile_edge[0]
    counts = tile_counts[0]
    slot = jnp.arange(tile_count, dtype=jnp.int32)[None, :]
    owner_idx = slot // slot_count
    slot_limit = jnp.sum(
        jnp.where(owner_idx == jnp.arange(groups, dtype=jnp.int32)[:, None], counts.T, 0),
        axis=0,
        keepdims=True,
    )
    live = slot % slot_count < slot_limit
    probs, probs_split = _softmax(logits, block_size)
    segments, halves = probs_split.shape[1], probs_split.shape[0]
    probs_half = probs_split.reshape(-1, block_size)
    split_idx = (pattern_idx % halves) * segments + pattern_idx // halves
    picked = jnp.take(probs_half, split_idx[0], axis=0, mode="clip")
    contrib = jnp.einsum("tq,tqe->te", picked, tile_block, preferred_element_type=jnp.float32)
    capacity_f = capacity.reshape(-1, block_size).astype(jnp.float32)
    owned_blocks = capacity_f.shape[0]
    idx_rows = -(-tile_count // block_size)
    rows_out = -(-(slot_count + idx_rows) // 8) * 8
    edge_f = jnp.full((1, idx_rows * block_size), -1.0, jnp.float32).at[:, :tile_count].set(
        jnp.where(live, edge_idx, -1).astype(jnp.float32)
    )
    payload = jnp.concatenate(
        [
            contrib.reshape(groups, slot_count, block_size),
            jnp.broadcast_to(edge_f.reshape(1, idx_rows, block_size), (groups, idx_rows, block_size)),
            jnp.zeros((groups, rows_out - slot_count - idx_rows, block_size), jnp.float32),
        ],
        axis=1,
    )
    received = lax.all_to_all(payload, "nets", 0, 0, tiled=False)
    every_edge = received[:, slot_count : slot_count + idx_rows].reshape(groups, -1)
    me = lax.axis_index("nets")
    asked = (
        lax.dynamic_slice_in_dim(every_edge, me * slot_count, slot_count, axis=1)
        .astype(jnp.int32)
        .reshape(1, -1)
    )
    usage_edges = _add_rows(asked, received[:, :slot_count].reshape(-1, block_size), owned_blocks)
    edge_grad = jax.nn.sigmoid(usage_edges - capacity_f).astype(jnp.bfloat16)
    answer = _take_rows(edge_grad, asked).reshape(groups, slot_count, block_size)
    slot_grads = lax.all_to_all(answer, "nets", 0, 0, tiled=False).reshape(-1, block_size)
    dp_tiles = jnp.einsum("tqe,te->tq", tile_block, slot_grads, preferred_element_type=jnp.float32)
    idx_rows = -(-tile_count // block_size)
    idx_f = jnp.full((1, idx_rows * block_size), -1.0, jnp.float32).at[:, :tile_count].set(
        jnp.where(live, split_idx, -1).astype(jnp.float32)
    )
    packed = jnp.concatenate([dp_tiles, idx_f.reshape(idx_rows, block_size)], axis=0)
    gathered = lax.all_gather(packed, "region", axis=0, tiled=False)
    all_dp = gathered[:, :tile_count].reshape(-1, block_size)
    all_idx = (
        gathered[:, tile_count:].reshape(gathered.shape[0], -1)[:, :tile_count]
        .astype(jnp.int32)
        .reshape(1, -1)
    )
    summed = _add_rows(all_idx, all_dp, probs_half.shape[0]).reshape(halves, segments, block_size)
    summed_grad = jnp.concatenate([summed[h] for h in range(halves)], axis=1)
    logit_grad = probs * (summed_grad - jnp.sum(probs * summed_grad, axis=-1, keepdims=True))
    return (logit_grad, usage_edges.reshape(capacity.shape))


def solution(mesh):
    in_specs = (
        P("nets", None),
        P("nets", "region", None, None, None),
        P("nets", "region", None),
        P("nets", "region", None),
        P("nets", "region", None),
        P("region", "nets"),
    )
    out_specs = (P("nets", None), P("region", "nets"))
    return jax.shard_map(shards, mesh=mesh, in_specs=in_specs, out_specs=out_specs, check_vma=False)
```

```python
import jax
import jax.numpy as jnp
from jax import lax
from jax.experimental import pallas as pl
from jax.sharding import PartitionSpec as P


def _one_hot_t(idx_row, size, dtype):
    return (jnp.arange(size, dtype=jnp.int32)[:, None] == idx_row).astype(dtype)


def _take_rows(table, idx_row):
    sel = _one_hot_t(idx_row, table.shape[0], table.dtype)
    out = lax.dot_general(sel, table, (((0,), (0,)), ((), ())), preferred_element_type=jnp.float32)
    return out.astype(table.dtype)


def _add_rows(idx_row, rows, size):
    hi = lax.reduce_precision(rows, exponent_bits=8, mantissa_bits=7)
    rest = rows - hi
    mid = lax.reduce_precision(rest, exponent_bits=8, mantissa_bits=7)
    lo = rest - mid
    parts = jnp.concatenate([hi, mid, lo], axis=1).astype(jnp.bfloat16)
    sel = _one_hot_t(idx_row, size, jnp.bfloat16)
    out = jnp.dot(sel, parts, preferred_element_type=jnp.float32)
    width = rows.shape[1]
    return out[:, :width] + out[:, width : 2 * width] + out[:, 2 * width :]


def _softmax_kernel(x_ref, p_ref, h_ref):
    x = x_ref[...]
    e = jnp.exp(x - jnp.max(x, axis=-1, keepdims=True))
    p = e * (1.0 / jnp.sum(e, axis=-1, keepdims=True))
    p_ref[...] = p
    half = p.astype(jnp.bfloat16)
    width = h_ref.shape[-1]
    for h in range(h_ref.shape[0]):
        h_ref[h] = half[:, h * width : (h + 1) * width]


def _softmax(logits, block_size):
    rows, width = logits.shape
    halves = width // block_size
    step = min(rows, 512)
    return pl.pallas_call(
        _softmax_kernel,
        grid=(rows // step,),
        in_specs=[pl.BlockSpec((step, width), lambda i: (i, 0))],
        out_specs=[
            pl.BlockSpec((step, width), lambda i: (i, 0)),
            pl.BlockSpec((halves, step, block_size), lambda i: (0, i, 0)),
        ],
        out_shape=[
            jax.ShapeDtypeStruct((rows, width), jnp.float32),
            jax.ShapeDtypeStruct((halves, rows, block_size), jnp.bfloat16),
        ],
        cost_estimate=pl.CostEstimate(
            flops=5 * rows * width, transcendentals=rows * width, bytes_accessed=10 * rows * width
        ),
    )(logits)


def shards(logits, tile_values, tile_pattern, tile_edge, tile_counts, capacity):
    groups = lax.axis_size("nets")
    tile_block = tile_values[0, 0]
    tile_count = tile_block.shape[0]
    block_size = tile_block.shape[1]
    slot_count = tile_count // groups
    pattern_idx = tile_pattern[0]
    edge_idx = tile_edge[0]
    counts = tile_counts[0]
    slot = jnp.arange(tile_count, dtype=jnp.int32)[None, :]
    slot_limit = jnp.broadcast_to(counts[0][:, None], (groups, slot_count)).reshape(1, tile_count)
    live = slot % slot_count < slot_limit
    probs, probs_split = _softmax(logits, block_size)
    segments, halves = probs_split.shape[1], probs_split.shape[0]
    probs_half = probs_split.reshape(-1, block_size)
    split_idx = (pattern_idx % halves) * segments + pattern_idx // halves
    picked = jnp.take(probs_half, split_idx[0], axis=0, mode="clip")
    contrib = jnp.einsum("tq,tqe->te", picked, tile_block, preferred_element_type=jnp.float32)
    capacity_f = capacity.reshape(-1, block_size).astype(jnp.float32)
    owned_blocks = capacity_f.shape[0]
    idx_rows = -(-tile_count // block_size)
    rows_out = -(-(slot_count + idx_rows) // 8) * 8
    edge_f = jnp.full((1, idx_rows * block_size), -1.0, jnp.float32).at[:, :tile_count].set(
        jnp.where(live, edge_idx, -1).astype(jnp.float32)
    )
    payload = jnp.concatenate(
        [
            contrib.reshape(groups, slot_count, block_size),
            jnp.broadcast_to(edge_f.reshape(1, idx_rows, block_size), (groups, idx_rows, block_size)),
            jnp.zeros((groups, rows_out - slot_count - idx_rows, block_size), jnp.float32),
        ],
        axis=1,
    )
    received = lax.all_to_all(payload, "nets", 0, 0, tiled=False)
    every_edge = received[:, slot_count : slot_count + idx_rows].reshape(groups, -1)
    me = lax.axis_index("nets")
    asked = (
        lax.dynamic_slice_in_dim(every_edge, me * slot_count, slot_count, axis=1)
        .astype(jnp.int32)
        .reshape(1, -1)
    )
    usage_edges = _add_rows(asked, received[:, :slot_count].reshape(-1, block_size), owned_blocks)
    edge_grad = jax.nn.sigmoid(usage_edges - capacity_f).astype(jnp.bfloat16)
    answer = _take_rows(edge_grad, asked).reshape(groups, slot_count, block_size)
    slot_grads = lax.all_to_all(answer, "nets", 0, 0, tiled=False).reshape(-1, block_size)
    dp_tiles = jnp.einsum("tqe,te->tq", tile_block, slot_grads, preferred_element_type=jnp.float32)
    idx_rows = -(-tile_count // block_size)
    idx_f = jnp.full((1, idx_rows * block_size), -1.0, jnp.float32).at[:, :tile_count].set(
        jnp.where(live, split_idx, -1).astype(jnp.float32)
    )
    packed = jnp.concatenate([dp_tiles, idx_f.reshape(idx_rows, block_size)], axis=0)
    gathered = lax.all_gather(packed, "region", axis=0, tiled=False)
    all_dp = gathered[:, :tile_count].reshape(-1, block_size)
    all_idx = (
        gathered[:, tile_count:].reshape(gathered.shape[0], -1)[:, :tile_count]
        .astype(jnp.int32)
        .reshape(1, -1)
    )
    summed = _add_rows(all_idx, all_dp, probs_half.shape[0]).reshape(halves, segments, block_size)
    summed_grad = jnp.concatenate([summed[h] for h in range(halves)], axis=1)
    logit_grad = probs * (summed_grad - jnp.sum(probs * summed_grad, axis=-1, keepdims=True))
    return (logit_grad, usage_edges.reshape(capacity.shape))


def solution(mesh):
    in_specs = (
        P("nets", None),
        P("nets", "region", None, None, None),
        P("nets", "region", None),
        P("nets", "region", None),
        P("nets", "region", None),
        P("region", "nets"),
    )
    out_specs = (P("nets", None), P("region", "nets"))
    return jax.shard_map(shards, mesh=mesh, in_specs=in_specs, out_specs=out_specs, check_vma=False)
```

```python
import jax
import jax.numpy as jnp
from jax import lax
from jax.experimental import pallas as pl
from jax.sharding import PartitionSpec as P


def _one_hot_t(idx_row, size, dtype):
    return (jnp.arange(size, dtype=jnp.int32)[:, None] == idx_row).astype(dtype)


def _take_rows(table, idx_row):
    sel = _one_hot_t(idx_row, table.shape[0], table.dtype)
    out = lax.dot_general(sel, table, (((0,), (0,)), ((), ())), preferred_element_type=jnp.float32)
    return out.astype(table.dtype)


def _add_rows(idx_row, rows, size):
    hi = lax.reduce_precision(rows, exponent_bits=8, mantissa_bits=7)
    rest = rows - hi
    mid = lax.reduce_precision(rest, exponent_bits=8, mantissa_bits=7)
    lo = rest - mid
    parts = jnp.concatenate([hi, mid, lo], axis=1).astype(jnp.bfloat16)
    sel = _one_hot_t(idx_row, size, jnp.bfloat16)
    out = jnp.dot(sel, parts, preferred_element_type=jnp.float32)
    width = rows.shape[1]
    return out[:, :width] + out[:, width : 2 * width] + out[:, 2 * width :]


def _softmax_kernel(x_ref, p_ref):
    x = x_ref[...]
    e = jnp.exp(x - jnp.max(x, axis=-1, keepdims=True))
    p_ref[...] = e * (1.0 / jnp.sum(e, axis=-1, keepdims=True))


def _softmax(logits):
    rows, width = logits.shape
    step = min(rows, 512)
    return pl.pallas_call(
        _softmax_kernel,
        grid=(rows // step,),
        in_specs=[pl.BlockSpec((step, width), lambda i: (i, 0))],
        out_specs=pl.BlockSpec((step, width), lambda i: (i, 0)),
        out_shape=jax.ShapeDtypeStruct((rows, width), jnp.float32),
        cost_estimate=pl.CostEstimate(
            flops=5 * rows * width, transcendentals=rows * width, bytes_accessed=8 * rows * width
        ),
    )(logits)


def shards(logits, tile_values, tile_pattern, tile_edge, tile_counts, capacity):
    groups = lax.axis_size("nets")
    tile_block = tile_values[0, 0]
    tile_count = tile_block.shape[0]
    block_size = tile_block.shape[1]
    slot_count = tile_count // groups
    pattern_idx = tile_pattern[0]
    edge_idx = tile_edge[0]
    counts = tile_counts[0]
    slot = jnp.arange(tile_count, dtype=jnp.int32)[None, :]
    owner_idx = slot // slot_count
    slot_limit = jnp.sum(
        jnp.where(owner_idx == jnp.arange(groups, dtype=jnp.int32)[:, None], counts.T, 0),
        axis=0,
        keepdims=True,
    )
    live = slot % slot_count < slot_limit
    probs = _softmax(logits)
    segments, halves = logits.shape[0], logits.shape[1] // block_size
    rows_sel = jnp.take(probs, pattern_idx[0] // halves, axis=0, mode="clip")
    rows_sel = rows_sel.reshape(tile_count, halves, block_size)
    which = (pattern_idx[0] % halves)[:, None, None] == jnp.arange(halves)[None, :, None]
    picked = jnp.sum(jnp.where(which, rows_sel, 0.0), axis=1).astype(jnp.bfloat16)
    split_idx = (pattern_idx % halves) * segments + pattern_idx // halves
    contrib = jnp.einsum("tq,tqe->te", picked, tile_block, preferred_element_type=jnp.float32)
    capacity_f = capacity.reshape(-1, block_size).astype(jnp.float32)
    owned_blocks = capacity_f.shape[0]
    idx_rows = -(-tile_count // block_size)
    rows_out = -(-(slot_count + idx_rows) // 8) * 8
    edge_f = jnp.full((1, idx_rows * block_size), -1.0, jnp.float32).at[:, :tile_count].set(
        jnp.where(live, edge_idx, -1).astype(jnp.float32)
    )
    payload = jnp.concatenate(
        [
            contrib.reshape(groups, slot_count, block_size),
            jnp.broadcast_to(edge_f.reshape(1, idx_rows, block_size), (groups, idx_rows, block_size)),
            jnp.zeros((groups, rows_out - slot_count - idx_rows, block_size), jnp.float32),
        ],
        axis=1,
    )
    received = lax.all_to_all(payload, "nets", 0, 0, tiled=False)
    every_edge = received[:, slot_count : slot_count + idx_rows].reshape(groups, -1)
    me = lax.axis_index("nets")
    asked = (
        lax.dynamic_slice_in_dim(every_edge, me * slot_count, slot_count, axis=1)
        .astype(jnp.int32)
        .reshape(1, -1)
    )
    usage_edges = _add_rows(asked, received[:, :slot_count].reshape(-1, block_size), owned_blocks)
    edge_grad = jax.nn.sigmoid(usage_edges - capacity_f).astype(jnp.bfloat16)
    answer = _take_rows(edge_grad, asked).reshape(groups, slot_count, block_size)
    slot_grads = lax.all_to_all(answer, "nets", 0, 0, tiled=False).reshape(-1, block_size)
    dp_tiles = jnp.einsum("tqe,te->tq", tile_block, slot_grads, preferred_element_type=jnp.float32)
    idx_rows = -(-tile_count // block_size)
    idx_f = jnp.full((1, idx_rows * block_size), -1.0, jnp.float32).at[:, :tile_count].set(
        jnp.where(live, split_idx, -1).astype(jnp.float32)
    )
    packed = jnp.concatenate([dp_tiles, idx_f.reshape(idx_rows, block_size)], axis=0)
    gathered = lax.all_gather(packed, "region", axis=0, tiled=False)
    all_dp = gathered[:, :tile_count].reshape(-1, block_size)
    all_idx = (
        gathered[:, tile_count:].reshape(gathered.shape[0], -1)[:, :tile_count]
        .astype(jnp.int32)
        .reshape(1, -1)
    )
    summed = _add_rows(all_idx, all_dp, halves * segments).reshape(halves, segments, block_size)
    summed_grad = jnp.concatenate([summed[h] for h in range(halves)], axis=1)
    logit_grad = probs * (summed_grad - jnp.sum(probs * summed_grad, axis=-1, keepdims=True))
    return (logit_grad, usage_edges.reshape(capacity.shape))


def solution(mesh):
    in_specs = (
        P("nets", None),
        P("nets", "region", None, None, None),
        P("nets", "region", None),
        P("nets", "region", None),
        P("nets", "region", None),
        P("region", "nets"),
    )
    out_specs = (P("nets", None), P("region", "nets"))
    return jax.shard_map(shards, mesh=mesh, in_specs=in_specs, out_specs=out_specs, check_vma=False)
```

```python
import jax
import jax.numpy as jnp
from jax import lax
from jax.experimental import pallas as pl
from jax.sharding import PartitionSpec as P


def _one_hot_t(idx_row, size, dtype):
    return (jnp.arange(size, dtype=jnp.int32)[:, None] == idx_row).astype(dtype)


def _take_rows(table, idx_row):
    sel = _one_hot_t(idx_row, table.shape[0], table.dtype)
    out = lax.dot_general(sel, table, (((0,), (0,)), ((), ())), preferred_element_type=jnp.float32)
    return out.astype(table.dtype)


def _add_rows(idx_row, rows, size):
    hi = lax.reduce_precision(rows, exponent_bits=8, mantissa_bits=7)
    rest = rows - hi
    mid = lax.reduce_precision(rest, exponent_bits=8, mantissa_bits=7)
    lo = rest - mid
    parts = jnp.concatenate([hi, mid, lo], axis=1).astype(jnp.bfloat16)
    sel = _one_hot_t(idx_row, size, jnp.bfloat16)
    out = jnp.dot(sel, parts, preferred_element_type=jnp.float32)
    width = rows.shape[1]
    return out[:, :width] + out[:, width : 2 * width] + out[:, 2 * width :]


def _softmax_kernel(x_ref, p_ref, h_ref):
    x = x_ref[...]
    e = jnp.exp(x - jnp.max(x, axis=-1, keepdims=True))
    p = e * (1.0 / jnp.sum(e, axis=-1, keepdims=True))
    p_ref[...] = p
    half = p.astype(jnp.bfloat16)
    width = h_ref.shape[-1]
    for h in range(h_ref.shape[0]):
        h_ref[h] = half[:, h * width : (h + 1) * width]


def _softmax(logits, block_size):
    rows, width = logits.shape
    halves = width // block_size
    step = min(rows, 256)
    return pl.pallas_call(
        _softmax_kernel,
        grid=(rows // step,),
        in_specs=[pl.BlockSpec((step, width), lambda i: (i, 0))],
        out_specs=[
            pl.BlockSpec((step, width), lambda i: (i, 0)),
            pl.BlockSpec((halves, step, block_size), lambda i: (0, i, 0)),
        ],
        out_shape=[
            jax.ShapeDtypeStruct((rows, width), jnp.float32),
            jax.ShapeDtypeStruct((halves, rows, block_size), jnp.bfloat16),
        ],
        cost_estimate=pl.CostEstimate(
            flops=5 * rows * width, transcendentals=rows * width, bytes_accessed=10 * rows * width
        ),
    )(logits)


def shards(logits, tile_values, tile_pattern, tile_edge, tile_counts, capacity):
    groups = lax.axis_size("nets")
    tile_block = tile_values[0, 0]
    tile_count = tile_block.shape[0]
    block_size = tile_block.shape[1]
    slot_count = tile_count // groups
    pattern_idx = tile_pattern[0]
    edge_idx = tile_edge[0]
    counts = tile_counts[0]
    slot = jnp.arange(tile_count, dtype=jnp.int32)[None, :]
    owner_idx = slot // slot_count
    slot_limit = jnp.sum(
        jnp.where(owner_idx == jnp.arange(groups, dtype=jnp.int32)[:, None], counts.T, 0),
        axis=0,
        keepdims=True,
    )
    live = slot % slot_count < slot_limit
    probs, probs_split = _softmax(logits, block_size)
    segments, halves = probs_split.shape[1], probs_split.shape[0]
    probs_half = probs_split.reshape(-1, block_size)
    split_idx = (pattern_idx % halves) * segments + pattern_idx // halves
    picked = jnp.take(probs_half, split_idx[0], axis=0, mode="clip")
    contrib = jnp.einsum("tq,tqe->te", picked, tile_block, preferred_element_type=jnp.float32)
    capacity_f = capacity.reshape(-1, block_size).astype(jnp.float32)
    owned_blocks = capacity_f.shape[0]
    idx_rows = -(-tile_count // block_size)
    rows_out = -(-(slot_count + idx_rows) // 8) * 8
    edge_f = jnp.full((1, idx_rows * block_size), -1.0, jnp.float32).at[:, :tile_count].set(
        jnp.where(live, edge_idx, -1).astype(jnp.float32)
    )
    payload = jnp.concatenate(
        [
            contrib.reshape(groups, slot_count, block_size),
            jnp.broadcast_to(edge_f.reshape(1, idx_rows, block_size), (groups, idx_rows, block_size)),
            jnp.zeros((groups, rows_out - slot_count - idx_rows, block_size), jnp.float32),
        ],
        axis=1,
    )
    received = lax.all_to_all(payload, "nets", 0, 0, tiled=False)
    every_edge = received[:, slot_count : slot_count + idx_rows].reshape(groups, -1)
    me = lax.axis_index("nets")
    asked = (
        lax.dynamic_slice_in_dim(every_edge, me * slot_count, slot_count, axis=1)
        .astype(jnp.int32)
        .reshape(1, -1)
    )
    usage_edges = _add_rows(asked, received[:, :slot_count].reshape(-1, block_size), owned_blocks)
    edge_grad = jax.nn.sigmoid(usage_edges - capacity_f).astype(jnp.bfloat16)
    answer = _take_rows(edge_grad, asked).reshape(groups, slot_count, block_size)
    slot_grads = lax.all_to_all(answer, "nets", 0, 0, tiled=False).reshape(-1, block_size)
    dp_tiles = jnp.einsum("tqe,te->tq", tile_block, slot_grads, preferred_element_type=jnp.float32)
    idx_rows = -(-tile_count // block_size)
    idx_f = jnp.full((1, idx_rows * block_size), -1.0, jnp.float32).at[:, :tile_count].set(
        jnp.where(live, split_idx, -1).astype(jnp.float32)
    )
    packed = jnp.concatenate([dp_tiles, idx_f.reshape(idx_rows, block_size)], axis=0)
    gathered = lax.all_gather(packed, "region", axis=0, tiled=False)
    all_dp = gathered[:, :tile_count].reshape(-1, block_size)
    all_idx = (
        gathered[:, tile_count:].reshape(gathered.shape[0], -1)[:, :tile_count]
        .astype(jnp.int32)
        .reshape(1, -1)
    )
    summed = _add_rows(all_idx, all_dp, probs_half.shape[0]).reshape(halves, segments, block_size)
    summed_grad = jnp.concatenate([summed[h] for h in range(halves)], axis=1)
    logit_grad = probs * (summed_grad - jnp.sum(probs * summed_grad, axis=-1, keepdims=True))
    return (logit_grad, usage_edges.reshape(capacity.shape))


def solution(mesh):
    in_specs = (
        P("nets", None),
        P("nets", "region", None, None, None),
        P("nets", "region", None),
        P("nets", "region", None),
        P("nets", "region", None),
        P("region", "nets"),
    )
    out_specs = (P("nets", None), P("region", "nets"))
    return jax.shard_map(shards, mesh=mesh, in_specs=in_specs, out_specs=out_specs, check_vma=False)
```

```python
import jax
import jax.numpy as jnp
from jax import lax
from jax.experimental import pallas as pl
from jax.sharding import PartitionSpec as P


def _one_hot_t(idx_row, size, dtype):
    return (jnp.arange(size, dtype=jnp.int32)[:, None] == idx_row).astype(dtype)


def _take_rows(table, idx_row):
    sel = _one_hot_t(idx_row, table.shape[0], table.dtype)
    out = lax.dot_general(sel, table, (((0,), (0,)), ((), ())), preferred_element_type=jnp.float32)
    return out.astype(table.dtype)


def _add_rows(idx_row, rows, size):
    hi = lax.reduce_precision(rows, exponent_bits=8, mantissa_bits=7)
    rest = rows - hi
    mid = lax.reduce_precision(rest, exponent_bits=8, mantissa_bits=7)
    lo = rest - mid
    parts = jnp.concatenate([hi, mid, lo], axis=1).astype(jnp.bfloat16)
    sel = _one_hot_t(idx_row, size, jnp.bfloat16)
    out = jnp.dot(sel, parts, preferred_element_type=jnp.float32)
    width = rows.shape[1]
    return out[:, :width] + out[:, width : 2 * width] + out[:, 2 * width :]


def _softmax_kernel(x_ref, p_ref):
    x = x_ref[...]
    e = jnp.exp(x - jnp.max(x, axis=-1, keepdims=True))
    p_ref[...] = e * (1.0 / jnp.sum(e, axis=-1, keepdims=True))


def _softmax(logits):
    rows, width = logits.shape
    step = min(rows, 512)
    return pl.pallas_call(
        _softmax_kernel,
        grid=(rows // step,),
        in_specs=[pl.BlockSpec((step, width), lambda i: (i, 0))],
        out_specs=pl.BlockSpec((step, width), lambda i: (i, 0)),
        out_shape=jax.ShapeDtypeStruct((rows, width), jnp.float32),
        cost_estimate=pl.CostEstimate(
            flops=5 * rows * width, transcendentals=rows * width, bytes_accessed=8 * rows * width
        ),
    )(logits)


def shards(logits, tile_values, tile_pattern, tile_edge, tile_counts, capacity):
    groups = lax.axis_size("nets")
    tile_block = tile_values[0, 0]
    tile_count = tile_block.shape[0]
    block_size = tile_block.shape[1]
    slot_count = tile_count // groups
    pattern_idx = tile_pattern[0]
    edge_idx = tile_edge[0]
    counts = tile_counts[0]
    slot = jnp.arange(tile_count, dtype=jnp.int32)[None, :]
    owner_idx = slot // slot_count
    slot_limit = jnp.sum(
        jnp.where(owner_idx == jnp.arange(groups, dtype=jnp.int32)[:, None], counts.T, 0),
        axis=0,
        keepdims=True,
    )
    live = slot % slot_count < slot_limit
    probs = _softmax(logits)
    segments, halves = logits.shape[0], logits.shape[1] // block_size
    half = probs.astype(jnp.bfloat16)
    probs_half = jnp.concatenate(
        [half[:, h * block_size : (h + 1) * block_size] for h in range(halves)], axis=0
    )
    split_idx = (pattern_idx % halves) * segments + pattern_idx // halves
    picked = jnp.take(probs_half, split_idx[0], axis=0, mode="clip")
    contrib = jnp.einsum("tq,tqe->te", picked, tile_block, preferred_element_type=jnp.float32)
    capacity_f = capacity.reshape(-1, block_size).astype(jnp.float32)
    owned_blocks = capacity_f.shape[0]
    idx_rows = -(-tile_count // block_size)
    rows_out = -(-(slot_count + idx_rows) // 8) * 8
    edge_f = jnp.full((1, idx_rows * block_size), -1.0, jnp.float32).at[:, :tile_count].set(
        jnp.where(live, edge_idx, -1).astype(jnp.float32)
    )
    payload = jnp.concatenate(
        [
            contrib.reshape(groups, slot_count, block_size),
            jnp.broadcast_to(edge_f.reshape(1, idx_rows, block_size), (groups, idx_rows, block_size)),
            jnp.zeros((groups, rows_out - slot_count - idx_rows, block_size), jnp.float32),
        ],
        axis=1,
    )
    received = lax.all_to_all(payload, "nets", 0, 0, tiled=False)
    every_edge = received[:, slot_count : slot_count + idx_rows].reshape(groups, -1)
    me = lax.axis_index("nets")
    asked = (
        lax.dynamic_slice_in_dim(every_edge, me * slot_count, slot_count, axis=1)
        .astype(jnp.int32)
        .reshape(1, -1)
    )
    usage_edges = _add_rows(asked, received[:, :slot_count].reshape(-1, block_size), owned_blocks)
    edge_grad = jax.nn.sigmoid(usage_edges - capacity_f).astype(jnp.bfloat16)
    answer = _take_rows(edge_grad, asked).reshape(groups, slot_count, block_size)
    slot_grads = lax.all_to_all(answer, "nets", 0, 0, tiled=False).reshape(-1, block_size)
    dp_tiles = jnp.einsum("tqe,te->tq", tile_block, slot_grads, preferred_element_type=jnp.float32)
    idx_rows = -(-tile_count // block_size)
    idx_f = jnp.full((1, idx_rows * block_size), -1.0, jnp.float32).at[:, :tile_count].set(
        jnp.where(live, split_idx, -1).astype(jnp.float32)
    )
    packed = jnp.concatenate([dp_tiles, idx_f.reshape(idx_rows, block_size)], axis=0)
    gathered = lax.all_gather(packed, "region", axis=0, tiled=False)
    all_dp = gathered[:, :tile_count].reshape(-1, block_size)
    all_idx = (
        gathered[:, tile_count:].reshape(gathered.shape[0], -1)[:, :tile_count]
        .astype(jnp.int32)
        .reshape(1, -1)
    )
    summed = _add_rows(all_idx, all_dp, probs_half.shape[0]).reshape(halves, segments, block_size)
    summed_grad = jnp.concatenate([summed[h] for h in range(halves)], axis=1)
    logit_grad = probs * (summed_grad - jnp.sum(probs * summed_grad, axis=-1, keepdims=True))
    return (logit_grad, usage_edges.reshape(capacity.shape))


def solution(mesh):
    in_specs = (
        P("nets", None),
        P("nets", "region", None, None, None),
        P("nets", "region", None),
        P("nets", "region", None),
        P("nets", "region", None),
        P("region", "nets"),
    )
    out_specs = (P("nets", None), P("region", "nets"))
    return jax.shard_map(shards, mesh=mesh, in_specs=in_specs, out_specs=out_specs, check_vma=False)
```

```python
import jax
import jax.numpy as jnp
from jax import lax
from jax.experimental import pallas as pl
from jax.sharding import PartitionSpec as P


def _one_hot_t(idx_row, size, dtype):
    return (jnp.arange(size, dtype=jnp.int32)[:, None] == idx_row).astype(dtype)


def _take_rows(table, idx_row):
    sel = _one_hot_t(idx_row, table.shape[0], table.dtype)
    out = lax.dot_general(sel, table, (((0,), (0,)), ((), ())), preferred_element_type=jnp.float32)
    return out.astype(table.dtype)


def _add_rows(idx_row, rows, size):
    hi = lax.reduce_precision(rows, exponent_bits=8, mantissa_bits=7)
    rest = rows - hi
    mid = lax.reduce_precision(rest, exponent_bits=8, mantissa_bits=7)
    lo = rest - mid
    parts = jnp.concatenate([hi, mid, lo], axis=1).astype(jnp.bfloat16)
    sel = _one_hot_t(idx_row, size, jnp.bfloat16)
    out = jnp.dot(sel, parts, preferred_element_type=jnp.float32)
    width = rows.shape[1]
    return out[:, :width] + out[:, width : 2 * width] + out[:, 2 * width :]


def _softmax_kernel(x_ref, p_ref):
    x = x_ref[...]
    e = jnp.exp(x - jnp.max(x, axis=-1, keepdims=True))
    p_ref[...] = e * (1.0 / jnp.sum(e, axis=-1, keepdims=True))


def _softmax(logits):
    rows, width = logits.shape
    step = min(rows, 512)
    return pl.pallas_call(
        _softmax_kernel,
        grid=(rows // step,),
        in_specs=[pl.BlockSpec((step, width), lambda i: (i, 0))],
        out_specs=pl.BlockSpec((step, width), lambda i: (i, 0)),
        out_shape=jax.ShapeDtypeStruct((rows, width), jnp.float32),
        cost_estimate=pl.CostEstimate(
            flops=5 * rows * width, transcendentals=rows * width, bytes_accessed=8 * rows * width
        ),
    )(logits)


def shards(logits, tile_values, tile_pattern, tile_edge, tile_counts, capacity):
    groups = lax.axis_size("nets")
    tile_block = tile_values[0, 0]
    tile_count = tile_block.shape[0]
    block_size = tile_block.shape[1]
    slot_count = tile_count // groups
    pattern_idx = tile_pattern[0]
    edge_idx = tile_edge[0]
    counts = tile_counts[0]
    slot = jnp.arange(tile_count, dtype=jnp.int32)[None, :]
    owner_idx = slot // slot_count
    slot_limit = jnp.sum(
        jnp.where(owner_idx == jnp.arange(groups, dtype=jnp.int32)[:, None], counts.T, 0),
        axis=0,
        keepdims=True,
    )
    live = slot % slot_count < slot_limit
    probs = _softmax(logits)
    probs, pattern_idx = lax.optimization_barrier((probs, pattern_idx))
    segments, halves = logits.shape[0], logits.shape[1] // block_size
    half = probs.astype(jnp.bfloat16)
    probs_half = jnp.concatenate(
        [half[:, h * block_size : (h + 1) * block_size] for h in range(halves)], axis=0
    )
    split_idx = (pattern_idx % halves) * segments + pattern_idx // halves
    picked = jnp.take(probs_half, split_idx[0], axis=0, mode="clip")
    contrib = jnp.einsum("tq,tqe->te", picked, tile_block, preferred_element_type=jnp.float32)
    capacity_f = capacity.reshape(-1, block_size).astype(jnp.float32)
    owned_blocks = capacity_f.shape[0]
    idx_rows = -(-tile_count // block_size)
    rows_out = -(-(slot_count + idx_rows) // 8) * 8
    edge_f = jnp.full((1, idx_rows * block_size), -1.0, jnp.float32).at[:, :tile_count].set(
        jnp.where(live, edge_idx, -1).astype(jnp.float32)
    )
    payload = jnp.concatenate(
        [
            contrib.reshape(groups, slot_count, block_size),
            jnp.broadcast_to(edge_f.reshape(1, idx_rows, block_size), (groups, idx_rows, block_size)),
            jnp.zeros((groups, rows_out - slot_count - idx_rows, block_size), jnp.float32),
        ],
        axis=1,
    )
    received = lax.all_to_all(payload, "nets", 0, 0, tiled=False)
    every_edge = received[:, slot_count : slot_count + idx_rows].reshape(groups, -1)
    me = lax.axis_index("nets")
    asked = (
        lax.dynamic_slice_in_dim(every_edge, me * slot_count, slot_count, axis=1)
        .astype(jnp.int32)
        .reshape(1, -1)
    )
    usage_edges = _add_rows(asked, received[:, :slot_count].reshape(-1, block_size), owned_blocks)
    edge_grad = jax.nn.sigmoid(usage_edges - capacity_f).astype(jnp.bfloat16)
    answer = _take_rows(edge_grad, asked).reshape(groups, slot_count, block_size)
    slot_grads = lax.all_to_all(answer, "nets", 0, 0, tiled=False).reshape(-1, block_size)
    dp_tiles = jnp.einsum("tqe,te->tq", tile_block, slot_grads, preferred_element_type=jnp.float32)
    idx_rows = -(-tile_count // block_size)
    idx_f = jnp.full((1, idx_rows * block_size), -1.0, jnp.float32).at[:, :tile_count].set(
        jnp.where(live, split_idx, -1).astype(jnp.float32)
    )
    packed = jnp.concatenate([dp_tiles, idx_f.reshape(idx_rows, block_size)], axis=0)
    gathered = lax.all_gather(packed, "region", axis=0, tiled=False)
    all_dp = gathered[:, :tile_count].reshape(-1, block_size)
    all_idx = (
        gathered[:, tile_count:].reshape(gathered.shape[0], -1)[:, :tile_count]
        .astype(jnp.int32)
        .reshape(1, -1)
    )
    summed = _add_rows(all_idx, all_dp, probs_half.shape[0]).reshape(halves, segments, block_size)
    summed_grad = jnp.concatenate([summed[h] for h in range(halves)], axis=1)
    logit_grad = probs * (summed_grad - jnp.sum(probs * summed_grad, axis=-1, keepdims=True))
    return (logit_grad, usage_edges.reshape(capacity.shape))


def solution(mesh):
    in_specs = (
        P("nets", None),
        P("nets", "region", None, None, None),
        P("nets", "region", None),
        P("nets", "region", None),
        P("nets", "region", None),
        P("region", "nets"),
    )
    out_specs = (P("nets", None), P("region", "nets"))
    return jax.shard_map(shards, mesh=mesh, in_specs=in_specs, out_specs=out_specs, check_vma=False)
```

```python
import jax
import jax.numpy as jnp
from jax import lax
from jax.experimental import pallas as pl
from jax.sharding import PartitionSpec as P


def _one_hot_t(idx_row, size, dtype):
    return (jnp.arange(size, dtype=jnp.int32)[:, None] == idx_row).astype(dtype)


def _take_rows(table, idx_row):
    sel = _one_hot_t(idx_row, table.shape[0], table.dtype)
    out = lax.dot_general(sel, table, (((0,), (0,)), ((), ())), preferred_element_type=jnp.float32)
    return out.astype(table.dtype)


def _add_rows(idx_row, rows, size):
    hi = lax.reduce_precision(rows, exponent_bits=8, mantissa_bits=7)
    rest = rows - hi
    mid = lax.reduce_precision(rest, exponent_bits=8, mantissa_bits=7)
    lo = rest - mid
    parts = jnp.concatenate([hi, mid, lo], axis=1).astype(jnp.bfloat16)
    sel = _one_hot_t(idx_row, size, jnp.bfloat16)
    out = jnp.dot(sel, parts, preferred_element_type=jnp.float32)
    width = rows.shape[1]
    return out[:, :width] + out[:, width : 2 * width] + out[:, 2 * width :]


def _softmax_kernel(x_ref, p_ref):
    x = x_ref[...]
    e = jnp.exp(x - jnp.max(x, axis=-1, keepdims=True))
    p_ref[...] = e * (1.0 / jnp.sum(e, axis=-1, keepdims=True))


def _softmax(logits):
    rows, width = logits.shape
    step = min(rows, 512)
    return pl.pallas_call(
        _softmax_kernel,
        grid=(rows // step,),
        in_specs=[pl.BlockSpec((step, width), lambda i: (i, 0))],
        out_specs=pl.BlockSpec((step, width), lambda i: (i, 0)),
        out_shape=jax.ShapeDtypeStruct((rows, width), jnp.float32),
        cost_estimate=pl.CostEstimate(
            flops=5 * rows * width, transcendentals=rows * width, bytes_accessed=8 * rows * width
        ),
    )(logits)


def shards(logits, tile_values, tile_pattern, tile_edge, tile_counts, capacity):
    groups = lax.axis_size("nets")
    tile_block = tile_values[0, 0]
    tile_count = tile_block.shape[0]
    block_size = tile_block.shape[1]
    slot_count = tile_count // groups
    pattern_idx = tile_pattern[0]
    edge_idx = tile_edge[0]
    counts = tile_counts[0]
    slot = jnp.arange(tile_count, dtype=jnp.int32)[None, :]
    owner_idx = slot // slot_count
    slot_limit = jnp.sum(
        jnp.where(owner_idx == jnp.arange(groups, dtype=jnp.int32)[:, None], counts.T, 0),
        axis=0,
        keepdims=True,
    )
    live = slot % slot_count < slot_limit
    probs = _softmax(logits)
    segments, halves = logits.shape[0], logits.shape[1] // block_size
    half = probs.astype(jnp.bfloat16)
    probs_half = jnp.concatenate(
        [half[:, h * block_size : (h + 1) * block_size] for h in range(halves)], axis=0
    )
    split_idx = (pattern_idx % halves) * segments + pattern_idx // halves
    picked = _take_rows(probs_half, split_idx)
    contrib = jnp.einsum("tq,tqe->te", picked, tile_block, preferred_element_type=jnp.float32)
    capacity_f = capacity.reshape(-1, block_size).astype(jnp.float32)
    owned_blocks = capacity_f.shape[0]
    idx_rows = -(-tile_count // block_size)
    rows_out = -(-(slot_count + idx_rows) // 8) * 8
    edge_f = jnp.full((1, idx_rows * block_size), -1.0, jnp.float32).at[:, :tile_count].set(
        jnp.where(live, edge_idx, -1).astype(jnp.float32)
    )
    payload = jnp.concatenate(
        [
            contrib.reshape(groups, slot_count, block_size),
            jnp.broadcast_to(edge_f.reshape(1, idx_rows, block_size), (groups, idx_rows, block_size)),
            jnp.zeros((groups, rows_out - slot_count - idx_rows, block_size), jnp.float32),
        ],
        axis=1,
    )
    received = lax.all_to_all(payload, "nets", 0, 0, tiled=False)
    every_edge = received[:, slot_count : slot_count + idx_rows].reshape(groups, -1)
    me = lax.axis_index("nets")
    asked = (
        lax.dynamic_slice_in_dim(every_edge, me * slot_count, slot_count, axis=1)
        .astype(jnp.int32)
        .reshape(1, -1)
    )
    usage_edges = _add_rows(asked, received[:, :slot_count].reshape(-1, block_size), owned_blocks)
    edge_grad = jax.nn.sigmoid(usage_edges - capacity_f).astype(jnp.bfloat16)
    answer = _take_rows(edge_grad, asked).reshape(groups, slot_count, block_size)
    slot_grads = lax.all_to_all(answer, "nets", 0, 0, tiled=False).reshape(-1, block_size)
    dp_tiles = jnp.einsum("tqe,te->tq", tile_block, slot_grads, preferred_element_type=jnp.float32)
    idx_rows = -(-tile_count // block_size)
    idx_f = jnp.full((1, idx_rows * block_size), -1.0, jnp.float32).at[:, :tile_count].set(
        jnp.where(live, split_idx, -1).astype(jnp.float32)
    )
    packed = jnp.concatenate([dp_tiles, idx_f.reshape(idx_rows, block_size)], axis=0)
    gathered = lax.all_gather(packed, "region", axis=0, tiled=False)
    all_dp = gathered[:, :tile_count].reshape(-1, block_size)
    all_idx = (
        gathered[:, tile_count:].reshape(gathered.shape[0], -1)[:, :tile_count]
        .astype(jnp.int32)
        .reshape(1, -1)
    )
    summed = _add_rows(all_idx, all_dp, probs_half.shape[0]).reshape(halves, segments, block_size)
    summed_grad = jnp.concatenate([summed[h] for h in range(halves)], axis=1)
    logit_grad = probs * (summed_grad - jnp.sum(probs * summed_grad, axis=-1, keepdims=True))
    return (logit_grad, usage_edges.reshape(capacity.shape))


def solution(mesh):
    in_specs = (
        P("nets", None),
        P("nets", "region", None, None, None),
        P("nets", "region", None),
        P("nets", "region", None),
        P("nets", "region", None),
        P("region", "nets"),
    )
    out_specs = (P("nets", None), P("region", "nets"))
    return jax.shard_map(shards, mesh=mesh, in_specs=in_specs, out_specs=out_specs, check_vma=False)
```

```python
import jax
import jax.numpy as jnp
from jax import lax
from jax.experimental import pallas as pl
from jax.sharding import PartitionSpec as P


def _one_hot_t(idx_row, size, dtype):
    return (jnp.arange(size, dtype=jnp.int32)[:, None] == idx_row).astype(dtype)


def _take_rows(table, idx_row):
    sel = _one_hot_t(idx_row, table.shape[0], table.dtype)
    out = lax.dot_general(sel, table, (((0,), (0,)), ((), ())), preferred_element_type=jnp.float32)
    return out.astype(table.dtype)


def _add_rows(idx_row, rows, size):
    hi = lax.reduce_precision(rows, exponent_bits=8, mantissa_bits=7)
    rest = rows - hi
    mid = lax.reduce_precision(rest, exponent_bits=8, mantissa_bits=7)
    lo = rest - mid
    parts = jnp.concatenate([hi, mid, lo], axis=1).astype(jnp.bfloat16)
    sel = _one_hot_t(idx_row, size, jnp.bfloat16)
    out = jnp.dot(sel, parts, preferred_element_type=jnp.float32)
    width = rows.shape[1]
    return out[:, :width] + out[:, width : 2 * width] + out[:, 2 * width :]


def _softmax_kernel(x_ref, p_ref):
    x = x_ref[...]
    e = jnp.exp(x - jnp.max(x, axis=-1, keepdims=True))
    p_ref[...] = e * (1.0 / jnp.sum(e, axis=-1, keepdims=True))


def _softmax(logits):
    rows, width = logits.shape
    step = rows
    return pl.pallas_call(
        _softmax_kernel,
        grid=(rows // step,),
        in_specs=[pl.BlockSpec((step, width), lambda i: (i, 0))],
        out_specs=pl.BlockSpec((step, width), lambda i: (i, 0)),
        out_shape=jax.ShapeDtypeStruct((rows, width), jnp.float32),
        cost_estimate=pl.CostEstimate(
            flops=5 * rows * width, transcendentals=rows * width, bytes_accessed=8 * rows * width
        ),
    )(logits)


def shards(logits, tile_values, tile_pattern, tile_edge, tile_counts, capacity):
    groups = lax.axis_size("nets")
    tile_block = tile_values[0, 0]
    tile_count = tile_block.shape[0]
    block_size = tile_block.shape[1]
    slot_count = tile_count // groups
    pattern_idx = tile_pattern[0]
    edge_idx = tile_edge[0]
    counts = tile_counts[0]
    slot = jnp.arange(tile_count, dtype=jnp.int32)[None, :]
    owner_idx = slot // slot_count
    slot_limit = jnp.sum(
        jnp.where(owner_idx == jnp.arange(groups, dtype=jnp.int32)[:, None], counts.T, 0),
        axis=0,
        keepdims=True,
    )
    live = slot % slot_count < slot_limit
    probs = _softmax(logits)
    segments, halves = logits.shape[0], logits.shape[1] // block_size
    half = probs.astype(jnp.bfloat16)
    probs_half = jnp.concatenate(
        [half[:, h * block_size : (h + 1) * block_size] for h in range(halves)], axis=0
    )
    split_idx = (pattern_idx % halves) * segments + pattern_idx // halves
    picked = _take_rows(probs_half, split_idx)
    contrib = jnp.einsum("tq,tqe->te", picked, tile_block, preferred_element_type=jnp.float32)
    capacity_f = capacity.reshape(-1, block_size).astype(jnp.float32)
    owned_blocks = capacity_f.shape[0]
    idx_rows = -(-tile_count // block_size)
    rows_out = -(-(slot_count + idx_rows) // 8) * 8
    edge_f = jnp.full((1, idx_rows * block_size), -1.0, jnp.float32).at[:, :tile_count].set(
        jnp.where(live, edge_idx, -1).astype(jnp.float32)
    )
    payload = jnp.concatenate(
        [
            contrib.reshape(groups, slot_count, block_size),
            jnp.broadcast_to(edge_f.reshape(1, idx_rows, block_size), (groups, idx_rows, block_size)),
            jnp.zeros((groups, rows_out - slot_count - idx_rows, block_size), jnp.float32),
        ],
        axis=1,
    )
    received = lax.all_to_all(payload, "nets", 0, 0, tiled=False)
    every_edge = received[:, slot_count : slot_count + idx_rows].reshape(groups, -1)
    me = lax.axis_index("nets")
    asked = (
        lax.dynamic_slice_in_dim(every_edge, me * slot_count, slot_count, axis=1)
        .astype(jnp.int32)
        .reshape(1, -1)
    )
    usage_edges = _add_rows(asked, received[:, :slot_count].reshape(-1, block_size), owned_blocks)
    edge_grad = jax.nn.sigmoid(usage_edges - capacity_f).astype(jnp.bfloat16)
    answer = _take_rows(edge_grad, asked).reshape(groups, slot_count, block_size)
    slot_grads = lax.all_to_all(answer, "nets", 0, 0, tiled=False).reshape(-1, block_size)
    dp_tiles = jnp.einsum("tqe,te->tq", tile_block, slot_grads, preferred_element_type=jnp.float32)
    idx_rows = -(-tile_count // block_size)
    idx_f = jnp.full((1, idx_rows * block_size), -1.0, jnp.float32).at[:, :tile_count].set(
        jnp.where(live, split_idx, -1).astype(jnp.float32)
    )
    packed = jnp.concatenate([dp_tiles, idx_f.reshape(idx_rows, block_size)], axis=0)
    gathered = lax.all_gather(packed, "region", axis=0, tiled=False)
    all_dp = gathered[:, :tile_count].reshape(-1, block_size)
    all_idx = (
        gathered[:, tile_count:].reshape(gathered.shape[0], -1)[:, :tile_count]
        .astype(jnp.int32)
        .reshape(1, -1)
    )
    summed = _add_rows(all_idx, all_dp, probs_half.shape[0]).reshape(halves, segments, block_size)
    summed_grad = jnp.concatenate([summed[h] for h in range(halves)], axis=1)
    logit_grad = probs * (summed_grad - jnp.sum(probs * summed_grad, axis=-1, keepdims=True))
    return (logit_grad, usage_edges.reshape(capacity.shape))


def solution(mesh):
    in_specs = (
        P("nets", None),
        P("nets", "region", None, None, None),
        P("nets", "region", None),
        P("nets", "region", None),
        P("nets", "region", None),
        P("region", "nets"),
    )
    out_specs = (P("nets", None), P("region", "nets"))
    return jax.shard_map(shards, mesh=mesh, in_specs=in_specs, out_specs=out_specs, check_vma=False)
```

```python
import jax
import jax.numpy as jnp
from jax import lax
from jax.experimental import pallas as pl
from jax.sharding import PartitionSpec as P


def _one_hot_t(idx_row, size, dtype):
    return (jnp.arange(size, dtype=jnp.int32)[:, None] == idx_row).astype(dtype)


def _take_rows(table, idx_row):
    sel = _one_hot_t(idx_row, table.shape[0], table.dtype)
    out = lax.dot_general(sel, table, (((0,), (0,)), ((), ())), preferred_element_type=jnp.float32)
    return out.astype(table.dtype)


def _add_rows(idx_row, rows, size):
    hi = lax.reduce_precision(rows, exponent_bits=8, mantissa_bits=7)
    rest = rows - hi
    mid = lax.reduce_precision(rest, exponent_bits=8, mantissa_bits=7)
    lo = rest - mid
    parts = jnp.concatenate([hi, mid, lo], axis=1).astype(jnp.bfloat16)
    sel = _one_hot_t(idx_row, size, jnp.bfloat16)
    out = jnp.dot(sel, parts, preferred_element_type=jnp.float32)
    width = rows.shape[1]
    return out[:, :width] + out[:, width : 2 * width] + out[:, 2 * width :]


def _softmax_kernel(x_ref, p_ref):
    x = x_ref[...]
    e = jnp.exp(x - jnp.max(x, axis=-1, keepdims=True))
    p_ref[...] = e * (1.0 / jnp.sum(e, axis=-1, keepdims=True))


def _softmax(logits):
    rows, width = logits.shape
    step = min(rows, 512)
    return pl.pallas_call(
        _softmax_kernel,
        grid=(rows // step,),
        in_specs=[pl.BlockSpec((step, width), lambda i: (i, 0))],
        out_specs=pl.BlockSpec((step, width), lambda i: (i, 0)),
        out_shape=jax.ShapeDtypeStruct((rows, width), jnp.float32),
        cost_estimate=pl.CostEstimate(
            flops=5 * rows * width, transcendentals=rows * width, bytes_accessed=8 * rows * width
        ),
    )(logits)


def shards(logits, tile_values, tile_pattern, tile_edge, tile_counts, capacity):
    groups = lax.axis_size("nets")
    tile_block = tile_values[0, 0]
    tile_count = tile_block.shape[0]
    block_size = tile_block.shape[1]
    slot_count = tile_count // groups
    pattern_idx = tile_pattern[0]
    edge_idx = tile_edge[0]
    counts = tile_counts[0]
    slot = jnp.arange(tile_count, dtype=jnp.int32)[None, :]
    slot_limit = jnp.broadcast_to(counts[0][:, None], (groups, slot_count)).reshape(1, tile_count)
    live = slot % slot_count < slot_limit
    probs = _softmax(logits)
    segments, halves = logits.shape[0], logits.shape[1] // block_size
    half = probs.astype(jnp.bfloat16)
    probs_half = jnp.concatenate(
        [half[:, h * block_size : (h + 1) * block_size] for h in range(halves)], axis=0
    )
    split_idx = (pattern_idx % halves) * segments + pattern_idx // halves
    picked = _take_rows(probs_half, split_idx)
    contrib = jnp.einsum("tq,tqe->te", picked, tile_block, preferred_element_type=jnp.float32)
    capacity_f = capacity.reshape(-1, block_size).astype(jnp.float32)
    owned_blocks = capacity_f.shape[0]
    idx_rows = -(-tile_count // block_size)
    rows_out = -(-(slot_count + idx_rows) // 8) * 8
    edge_f = jnp.full((1, idx_rows * block_size), -1.0, jnp.float32).at[:, :tile_count].set(
        jnp.where(live, edge_idx, -1).astype(jnp.float32)
    )
    payload = jnp.concatenate(
        [
            contrib.reshape(groups, slot_count, block_size),
            jnp.broadcast_to(edge_f.reshape(1, idx_rows, block_size), (groups, idx_rows, block_size)),
            jnp.zeros((groups, rows_out - slot_count - idx_rows, block_size), jnp.float32),
        ],
        axis=1,
    )
    received = lax.all_to_all(payload, "nets", 0, 0, tiled=False)
    every_edge = received[:, slot_count : slot_count + idx_rows].reshape(groups, -1)
    me = lax.axis_index("nets")
    asked = (
        lax.dynamic_slice_in_dim(every_edge, me * slot_count, slot_count, axis=1)
        .astype(jnp.int32)
        .reshape(1, -1)
    )
    usage_edges = _add_rows(asked, received[:, :slot_count].reshape(-1, block_size), owned_blocks)
    edge_grad = jax.nn.sigmoid(usage_edges - capacity_f).astype(jnp.bfloat16)
    answer = _take_rows(edge_grad, asked).reshape(groups, slot_count, block_size)
    slot_grads = lax.all_to_all(answer, "nets", 0, 0, tiled=False).reshape(-1, block_size)
    dp_tiles = jnp.einsum("tqe,te->tq", tile_block, slot_grads, preferred_element_type=jnp.float32)
    idx_rows = -(-tile_count // block_size)
    idx_f = jnp.full((1, idx_rows * block_size), -1.0, jnp.float32).at[:, :tile_count].set(
        jnp.where(live, split_idx, -1).astype(jnp.float32)
    )
    packed = jnp.concatenate([dp_tiles, idx_f.reshape(idx_rows, block_size)], axis=0)
    gathered = lax.all_gather(packed, "region", axis=0, tiled=False)
    all_dp = gathered[:, :tile_count].reshape(-1, block_size)
    all_idx = (
        gathered[:, tile_count:].reshape(gathered.shape[0], -1)[:, :tile_count]
        .astype(jnp.int32)
        .reshape(1, -1)
    )
    summed = _add_rows(all_idx, all_dp, probs_half.shape[0]).reshape(halves, segments, block_size)
    summed_grad = jnp.concatenate([summed[h] for h in range(halves)], axis=1)
    logit_grad = probs * (summed_grad - jnp.sum(probs * summed_grad, axis=-1, keepdims=True))
    return (logit_grad, usage_edges.reshape(capacity.shape))


def solution(mesh):
    in_specs = (
        P("nets", None),
        P("nets", "region", None, None, None),
        P("nets", "region", None),
        P("nets", "region", None),
        P("nets", "region", None),
        P("region", "nets"),
    )
    out_specs = (P("nets", None), P("region", "nets"))
    return jax.shard_map(shards, mesh=mesh, in_specs=in_specs, out_specs=out_specs, check_vma=False)
```

```python
import jax
import jax.numpy as jnp
from jax import lax
from jax.experimental import pallas as pl
from jax.sharding import PartitionSpec as P


def _one_hot_t(idx_row, size, dtype):
    return (jnp.arange(size, dtype=jnp.int32)[:, None] == idx_row).astype(dtype)


def _take_rows(table, idx_row):
    sel = _one_hot_t(idx_row, table.shape[0], table.dtype)
    out = lax.dot_general(sel, table, (((0,), (0,)), ((), ())), preferred_element_type=jnp.float32)
    return out.astype(table.dtype)


def _add_rows(idx_row, rows, size):
    hi = lax.reduce_precision(rows, exponent_bits=8, mantissa_bits=7)
    rest = rows - hi
    mid = lax.reduce_precision(rest, exponent_bits=8, mantissa_bits=7)
    lo = rest - mid
    parts = jnp.concatenate([hi, mid, lo], axis=1).astype(jnp.bfloat16)
    sel = _one_hot_t(idx_row, size, jnp.bfloat16)
    out = jnp.dot(sel, parts, preferred_element_type=jnp.float32)
    width = rows.shape[1]
    return out[:, :width] + out[:, width : 2 * width] + out[:, 2 * width :]


def _softmax_kernel(x_ref, p_ref):
    x = x_ref[...]
    e = jnp.exp(x - jnp.max(x, axis=-1, keepdims=True))
    p_ref[...] = e * (1.0 / jnp.sum(e, axis=-1, keepdims=True))


def _softmax(logits):
    rows, width = logits.shape
    step = min(rows, 256)
    return pl.pallas_call(
        _softmax_kernel,
        grid=(rows // step,),
        in_specs=[pl.BlockSpec((step, width), lambda i: (i, 0))],
        out_specs=pl.BlockSpec((step, width), lambda i: (i, 0)),
        out_shape=jax.ShapeDtypeStruct((rows, width), jnp.float32),
        cost_estimate=pl.CostEstimate(
            flops=5 * rows * width, transcendentals=rows * width, bytes_accessed=8 * rows * width
        ),
    )(logits)


def shards(logits, tile_values, tile_pattern, tile_edge, tile_counts, capacity):
    groups = lax.axis_size("nets")
    tile_block = tile_values[0, 0]
    tile_count = tile_block.shape[0]
    block_size = tile_block.shape[1]
    slot_count = tile_count // groups
    pattern_idx = tile_pattern[0]
    edge_idx = tile_edge[0]
    counts = tile_counts[0]
    slot = jnp.arange(tile_count, dtype=jnp.int32)[None, :]
    owner_idx = slot // slot_count
    slot_limit = jnp.sum(
        jnp.where(owner_idx == jnp.arange(groups, dtype=jnp.int32)[:, None], counts.T, 0),
        axis=0,
        keepdims=True,
    )
    live = slot % slot_count < slot_limit
    probs = _softmax(logits)
    segments, halves = logits.shape[0], logits.shape[1] // block_size
    half = probs.astype(jnp.bfloat16)
    probs_half = jnp.concatenate(
        [half[:, h * block_size : (h + 1) * block_size] for h in range(halves)], axis=0
    )
    split_idx = (pattern_idx % halves) * segments + pattern_idx // halves
    picked = _take_rows(probs_half, split_idx)
    contrib = jnp.einsum("tq,tqe->te", picked, tile_block, preferred_element_type=jnp.float32)
    capacity_f = capacity.reshape(-1, block_size).astype(jnp.float32)
    owned_blocks = capacity_f.shape[0]
    idx_rows = -(-tile_count // block_size)
    rows_out = -(-(slot_count + idx_rows) // 8) * 8
    edge_f = jnp.full((1, idx_rows * block_size), -1.0, jnp.float32).at[:, :tile_count].set(
        jnp.where(live, edge_idx, -1).astype(jnp.float32)
    )
    payload = jnp.concatenate(
        [
            contrib.reshape(groups, slot_count, block_size),
            jnp.broadcast_to(edge_f.reshape(1, idx_rows, block_size), (groups, idx_rows, block_size)),
            jnp.zeros((groups, rows_out - slot_count - idx_rows, block_size), jnp.float32),
        ],
        axis=1,
    )
    received = lax.all_to_all(payload, "nets", 0, 0, tiled=False)
    every_edge = received[:, slot_count : slot_count + idx_rows].reshape(groups, -1)
    me = lax.axis_index("nets")
    asked = (
        lax.dynamic_slice_in_dim(every_edge, me * slot_count, slot_count, axis=1)
        .astype(jnp.int32)
        .reshape(1, -1)
    )
    usage_edges = _add_rows(asked, received[:, :slot_count].reshape(-1, block_size), owned_blocks)
    edge_grad = jax.nn.sigmoid(usage_edges - capacity_f).astype(jnp.bfloat16)
    answer = _take_rows(edge_grad, asked).reshape(groups, slot_count, block_size)
    slot_grads = lax.all_to_all(answer, "nets", 0, 0, tiled=False).reshape(-1, block_size)
    dp_tiles = jnp.einsum("tqe,te->tq", tile_block, slot_grads, preferred_element_type=jnp.float32)
    idx_rows = -(-tile_count // block_size)
    idx_f = jnp.full((1, idx_rows * block_size), -1.0, jnp.float32).at[:, :tile_count].set(
        jnp.where(live, split_idx, -1).astype(jnp.float32)
    )
    packed = jnp.concatenate([dp_tiles, idx_f.reshape(idx_rows, block_size)], axis=0)
    gathered = lax.all_gather(packed, "region", axis=0, tiled=False)
    all_dp = gathered[:, :tile_count].reshape(-1, block_size)
    all_idx = (
        gathered[:, tile_count:].reshape(gathered.shape[0], -1)[:, :tile_count]
        .astype(jnp.int32)
        .reshape(1, -1)
    )
    summed = _add_rows(all_idx, all_dp, probs_half.shape[0]).reshape(halves, segments, block_size)
    summed_grad = jnp.concatenate([summed[h] for h in range(halves)], axis=1)
    logit_grad = probs * (summed_grad - jnp.sum(probs * summed_grad, axis=-1, keepdims=True))
    return (logit_grad, usage_edges.reshape(capacity.shape))


def solution(mesh):
    in_specs = (
        P("nets", None),
        P("nets", "region", None, None, None),
        P("nets", "region", None),
        P("nets", "region", None),
        P("nets", "region", None),
        P("region", "nets"),
    )
    out_specs = (P("nets", None), P("region", "nets"))
    return jax.shard_map(shards, mesh=mesh, in_specs=in_specs, out_specs=out_specs, check_vma=False)
```
